512 devices in a mesh: dp: 64 (over z, y_hi, core), seq: 8 (over y_lo, x).
Axes of the slice: x: 4, y: 8 (y_hi: 4, y_lo: 2; y = y_hi * 2 + y_lo), z: 8, core: 2. Of those that a mesh axis runs over, the one named last changes fastest.
Arguments:
- tokens: bfloat16 [1024, 4096], P('seq', 'dp'), may hold values from -6 to 6
- in_weight: bfloat16 [2, 4096, 8192], P(None, 'seq', 'dp'), may hold values from -0.09375 to 0.09375
- conv_weight: bfloat16 [4, 8192], P(None, 'dp'), may hold values from -0.5 to 0.5
- conv_bias: bfloat16 [8192], P('dp'), may hold values from -1 to 1
- out_weight: bfloat16 [8192, 4096], P('dp', 'seq'), may hold values from -0.0625 to 0.0625
- grad_out: bfloat16 [1024, 4096], P('seq', 'dp'), may hold values from -6 to 6
Outputs:
- output: bfloat16 [1024, 4096], P('seq', 'dp')
- grad_tokens: bfloat16 [1024, 4096], P('seq', 'dp')
- grad_in_weight: float32 [2, 4096, 8192], P(None, 'seq', 'dp')
- grad_out_weight: float32 [8192, 4096], P('dp', 'seq')
- grad_conv_weight: float32 [4, 8192], P(None, 'dp')
- grad_conv_bias: float32 [8192], P('dp')
The draws below stay inside these ranges and needn't reach their ends.
All inputs are finite; a program needn't handle non-finite values.
Results may differ from the reference program's by a relative error of at most 0.012.
Values may be sent and summed in bfloat16 or wider, within the bound.
No kernel may reach another device: no remote copies, remote signals or barrier semaphores. Data moves between devices by JAX's collectives and lax.ppermute only.
A program may use at most 64 MiB of HBM per device.

```python
import jax
import jax.numpy as jnp
from jax import lax

D = 4096
E = 8192
KERNEL = 4
TOK_DEV = 128
TOKENS = 1024
N_SEQ = 8


def block_scale(rng, shape, cuts, low, top_value):
    def one(axis_at, parts):
        heights = jax.random.uniform(jax.random.fold_in(jax.random.fold_in(rng, 6), axis_at), (parts,), jnp.float32, low / len(cuts), top_value / len(cuts))
        return jnp.repeat(jnp.exp(heights), shape[axis_at] // parts).reshape((-1,) + (1,) * (len(shape) - axis_at - 1))

    level = one(*cuts[0])
    for cut in cuts[1:]:
        level = level * one(*cut)
    return level


def centred(own_key, extent, deviation, bound, shards=(), kind=jnp.bfloat16):
    result = jax.random.normal(own_key, extent, jnp.float32) * deviation
    if len(shards) > 0:
        result = block_scale(own_key, extent, shards, -0.22, 0.18) * result
    return jnp.clip(result, min=-bound, max=bound).astype(kind)


def setup_inputs(seed: int = 0) -> dict:
    keys = jax.random.split(jax.random.key(seed), 7)
    tokens = centred(keys[0], (TOKENS, D), 1.0, 6.0, ((0, 8), (1, 64)))
    in_weight = centred(keys[1], (2, D, E), D ** -0.5, 0.09375, ((1, 8), (2, 64)))
    conv_weight = jnp.clip(jax.random.uniform(keys[2], (KERNEL, E), jnp.float32, -0.5, 0.5) * block_scale(keys[2], (KERNEL, E), ((1, 64),), -0.4, 0.0), -0.5, 0.5).astype(jnp.bfloat16)
    conv_bias = jnp.clip(jax.random.uniform(keys[3], (E,), jnp.float32, -1.0, 1.0) * block_scale(keys[3], (E,), ((0, 64),), -0.4, 0.0), -1.0, 1.0).astype(jnp.bfloat16)
    out_weight = centred(keys[4], (E, D), E ** -0.5, 0.0625, ((0, 64), (1, 8)))
    grad_out = centred(keys[5], (TOKENS, D), 1.0, 6.0, ((0, 8), (1, 64)))
    return {"tokens": tokens, "in_weight": in_weight, "conv_weight": conv_weight, "conv_bias": conv_bias, "out_weight": out_weight, "grad_out": grad_out}


def silu_parts(value):
    sig = jax.nn.sigmoid(value)
    return value * sig, sig * (1.0 + value * (1.0 - sig))


def reference(tokens, in_weight, conv_weight, conv_bias, out_weight, grad_out):
    inner = jnp.dot(tokens, in_weight[0], preferred_element_type=jnp.float32).astype(jnp.bfloat16)
    gate_in = jnp.dot(tokens, in_weight[1], preferred_element_type=jnp.float32).astype(jnp.bfloat16)
    padded = jnp.concatenate([jnp.zeros((KERNEL - 1, E), jnp.bfloat16), inner], axis=0)
    conv = jnp.broadcast_to(conv_bias.astype(jnp.float32)[None, :], (TOKENS, E))
    for lag in range(KERNEL):
        conv = conv + conv_weight[lag].astype(jnp.float32)[None, :] * padded[lag:lag + TOKENS].astype(jnp.float32)
    act, act_slope = silu_parts(conv)
    gate, gate_slope = silu_parts(gate_in.astype(jnp.float32))
    hidden = (act * gate).astype(jnp.bfloat16)
    output = jnp.dot(hidden, out_weight, preferred_element_type=jnp.float32).astype(jnp.bfloat16)
    back = lax.dot_general(grad_out, out_weight, (((1,), (1,)), ((), ())), preferred_element_type=jnp.float32)
    grad_conv = (back * gate * act_slope).astype(jnp.bfloat16)
    grad_gate = (back * act * gate_slope).astype(jnp.bfloat16)
    ahead = jnp.concatenate([grad_conv, jnp.zeros((KERNEL - 1, E), jnp.bfloat16)], axis=0)
    grad_inner = jnp.zeros((TOKENS, E), jnp.float32)
    for lag in range(KERNEL):
        shift_start = KERNEL - 1 - lag
        grad_inner = grad_inner + conv_weight[lag].astype(jnp.float32)[None, :] * ahead[shift_start:shift_start + TOKENS].astype(jnp.float32)
    grad_inner = grad_inner.astype(jnp.bfloat16)
    grad_tokens = lax.dot_general(grad_inner, in_weight[0], (((1,), (1,)), ((), ())), preferred_element_type=jnp.float32)
    grad_tokens = grad_tokens + lax.dot_general(grad_gate, in_weight[1], (((1,), (1,)), ((), ())), preferred_element_type=jnp.float32)
    grad_tokens = grad_tokens.astype(jnp.bfloat16)
    conv_float = grad_conv.astype(jnp.float32)
    tap_rows = []
    for lag in range(KERNEL):
        tap_rows.append(jnp.sum(conv_float * padded[lag:lag + TOKENS].astype(jnp.float32), axis=0))
    grad_conv_weight = jnp.stack(tap_rows, axis=0)
    grad_conv_bias = jnp.sum(conv_float, axis=0)

    def accumulate(block, carry):
        sum_in, sum_out = carry
        first = (block * TOK_DEV).astype(jnp.int32)
        rows = lax.dynamic_slice_in_dim(tokens, first, TOK_DEV, 0)
        inner_rows = lax.dynamic_slice_in_dim(grad_inner, first, TOK_DEV, 0)
        gate_rows = lax.dynamic_slice_in_dim(grad_gate, first, TOK_DEV, 0)
        hidden_rows = lax.dynamic_slice_in_dim(hidden, first, TOK_DEV, 0)
        upstream_rows = lax.dynamic_slice_in_dim(grad_out, first, TOK_DEV, 0)
        term_inner = lax.dot_general(rows, inner_rows, (((0,), (0,)), ((), ())), preferred_element_type=jnp.float32)
        term_gate = lax.dot_general(rows, gate_rows, (((0,), (0,)), ((), ())), preferred_element_type=jnp.float32)
        term_in = jnp.stack([term_inner, term_gate], axis=0).astype(jnp.bfloat16).astype(jnp.float32)
        term_out = lax.dot_general(hidden_rows, upstream_rows, (((0,), (0,)), ((), ())), preferred_element_type=jnp.float32)
        term_out = term_out.astype(jnp.bfloat16).astype(jnp.float32)
        return sum_in + term_in, sum_out + term_out

    start_carry = (jnp.zeros((2, D, E), jnp.float32), jnp.zeros((E, D), jnp.float32))
    grad_in_weight, grad_out_weight = lax.fori_loop(0, N_SEQ, accumulate, start_carry)
    return output, grad_tokens, grad_in_weight, grad_out_weight, grad_conv_weight, grad_conv_bias
```

```python
import jax
import jax.numpy as jnp
from jax import lax
from jax.sharding import PartitionSpec as P


def from_behind(block, axis, distance):
    devices = range(lax.axis_size(axis))
    route = [(i - distance, i) for i in devices if i - distance in devices]
    return lax.ppermute(block, axis, route)


def silu_parts(value):
    sig = jax.nn.sigmoid(value)
    return (value * sig, sig * (1.0 + value * (1.0 - sig)))


def on_device(tokens, in_weight, conv_weight, conv_bias, out_weight, grad_out):
    w_local = jnp.concatenate([in_weight, out_weight.T[None]], axis=0)
    w_full = lax.all_gather(w_local, "seq", axis=1, tiled=True)
    in_full = w_full[:2]
    out_full_t = w_full[2]
    acts = jnp.stack([tokens, grad_out], axis=1)
    acts_full = lax.all_gather(acts, "dp", axis=2, tiled=True)
    whole = acts_full[:, 0]
    upstream = acts_full[:, 1]
    tok_rows = whole.shape[0]
    taps = conv_weight.shape[0]
    mixed = jnp.einsum("td,pde->tpe", whole, in_full, preferred_element_type=jnp.float32).astype(
        jnp.bfloat16
    )
    inner = mixed[:, 0, :]
    gate_in = mixed[:, 1, :]
    rim = from_behind(inner[tok_rows - (taps - 1) :], "seq", 1)
    padded = jnp.concatenate([rim, inner], axis=0)
    conv = jnp.broadcast_to(conv_bias.astype(jnp.float32)[None, :], inner.shape)
    for lag in range(taps):
        conv = conv + conv_weight[lag].astype(jnp.float32)[None, :] * padded[
            lag : lag + tok_rows
        ].astype(jnp.float32)
    act, act_slope = silu_parts(conv)
    gate, gate_slope = silu_parts(gate_in.astype(jnp.float32))
    hidden = (act * gate).astype(jnp.bfloat16)
    out_part = jnp.einsum("te,de->dt", hidden, out_full_t, preferred_element_type=jnp.float32)
    back = jnp.einsum("td,de->te", upstream, out_full_t, preferred_element_type=jnp.float32)
    grad_conv = (back * gate * act_slope).astype(jnp.bfloat16)
    grad_gate = (back * act * gate_slope).astype(jnp.bfloat16)
    ahead_rim = from_behind(grad_conv[: taps - 1], "seq", -1)
    ahead = jnp.concatenate([grad_conv, ahead_rim], axis=0)
    grad_inner = jnp.zeros(inner.shape, jnp.float32)
    for lag in range(taps):
        shift_start = taps - 1 - lag
        grad_inner = grad_inner + conv_weight[lag].astype(jnp.float32)[None, :] * ahead[
            shift_start : shift_start + tok_rows
        ].astype(jnp.float32)
    grad_inner = grad_inner.astype(jnp.bfloat16)
    conv_float = grad_conv.astype(jnp.float32)
    tap_rows = []
    for lag in range(taps):
        tap_rows.append(
            jnp.sum(conv_float * padded[lag : lag + tok_rows].astype(jnp.float32), axis=0)
        )
    tap_grads, bias_grads = lax.psum(
        (jnp.stack(tap_rows, axis=0), jnp.sum(conv_float, axis=0)), "seq"
    )
    branch_grads = jnp.stack([grad_inner, grad_gate], axis=1)
    tok_part = jnp.einsum("tpe,pde->dt", branch_grads, in_full, preferred_element_type=jnp.float32)
    reduced = lax.psum_scatter(
        jnp.stack([out_part, tok_part], axis=1), "dp", scatter_dimension=0, tiled=True
    )
    reduced = lax.optimization_barrier(reduced)
    output = reduced[:, 0].T.astype(jnp.bfloat16)
    grad_tokens = reduced[:, 1].T.astype(jnp.bfloat16)
    term_in = jnp.einsum("td,tpe->pde", whole, branch_grads, preferred_element_type=jnp.float32)
    term_out_t = jnp.einsum("td,te->de", upstream, hidden, preferred_element_type=jnp.float32)
    terms = jnp.concatenate([term_in, term_out_t[None]], axis=0).astype(jnp.bfloat16)
    terms = lax.psum_scatter(terms, "seq", scatter_dimension=1, tiled=True).astype(jnp.float32)
    grad_in_weight = terms[:2]
    grad_out_weight = terms[2].T
    return (output, grad_tokens, grad_in_weight, grad_out_weight, tap_grads, bias_grads)


def solution(mesh):
    return jax.shard_map(
        on_device,
        mesh=mesh,
        in_specs=(
            P("seq", "dp"),
            P(None, "seq", "dp"),
            P(None, "dp"),
            P("dp"),
            P("dp", "seq"),
            P("seq", "dp"),
        ),
        out_specs=(
            P("seq", "dp"),
            P("seq", "dp"),
            P(None, "seq", "dp"),
            P("dp", "seq"),
            P(None, "dp"),
            P("dp"),
        ),
        check_vma=False,
    )
```

```python
import jax
import jax.numpy as jnp
from jax import lax
from jax.sharding import PartitionSpec as P


def from_behind(block, axis, distance):
    devices = range(lax.axis_size(axis))
    route = [(i - distance, i) for i in devices if i - distance in devices]
    return lax.ppermute(block, axis, route)


def silu_parts(value):
    sig = jax.nn.sigmoid(value)
    return (value * sig, sig * (1.0 + value * (1.0 - sig)))


def on_device(tokens, in_weight, conv_weight, conv_bias, out_weight, grad_out):
    n_seq = lax.axis_size("seq")
    n_dp = lax.axis_size("dp")
    w_local = jnp.concatenate([in_weight, out_weight.T[None]], axis=0)
    w_rep = jnp.broadcast_to(w_local[None], (n_seq,) + w_local.shape)
    w_full = lax.all_to_all(w_rep, "seq", 0, 2, tiled=True)[0]
    in_full = w_full[:2]
    out_full_t = w_full[2]
    acts = jnp.stack([tokens, grad_out], axis=1)
    acts_full = lax.all_gather(acts, "dp", axis=2, tiled=True)
    whole = acts_full[:, 0]
    upstream = acts_full[:, 1]
    tok_rows = whole.shape[0]
    taps = conv_weight.shape[0]
    mixed = jnp.einsum("td,pde->tpe", whole, in_full, preferred_element_type=jnp.float32).astype(
        jnp.bfloat16
    )
    inner = mixed[:, 0, :]
    gate_in = mixed[:, 1, :]
    rim = from_behind(inner[tok_rows - (taps - 1) :], "seq", 1)
    padded = jnp.concatenate([rim, inner], axis=0)
    conv = jnp.broadcast_to(conv_bias.astype(jnp.float32)[None, :], inner.shape)
    for lag in range(taps):
        conv = conv + conv_weight[lag].astype(jnp.float32)[None, :] * padded[
            lag : lag + tok_rows
        ].astype(jnp.float32)
    act, act_slope = silu_parts(conv)
    gate, gate_slope = silu_parts(gate_in.astype(jnp.float32))
    hidden = (act * gate).astype(jnp.bfloat16)
    out_part = jnp.einsum("te,de->dt", hidden, out_full_t, preferred_element_type=jnp.float32)
    back = jnp.einsum("td,de->te", upstream, out_full_t, preferred_element_type=jnp.float32)
    grad_conv = (back * gate * act_slope).astype(jnp.bfloat16)
    grad_gate = (back * act * gate_slope).astype(jnp.bfloat16)
    ahead_rim = from_behind(grad_conv[: taps - 1], "seq", -1)
    ahead = jnp.concatenate([grad_conv, ahead_rim], axis=0)
    grad_inner = jnp.zeros(inner.shape, jnp.float32)
    for lag in range(taps):
        shift_start = taps - 1 - lag
        grad_inner = grad_inner + conv_weight[lag].astype(jnp.float32)[None, :] * ahead[
            shift_start : shift_start + tok_rows
        ].astype(jnp.float32)
    grad_inner = grad_inner.astype(jnp.bfloat16)
    conv_float = grad_conv.astype(jnp.float32)
    tap_rows = []
    for lag in range(taps):
        tap_rows.append(
            jnp.sum(conv_float * padded[lag : lag + tok_rows].astype(jnp.float32), axis=0)
        )
    tap_grads, bias_grads = lax.psum(
        (jnp.stack(tap_rows, axis=0), jnp.sum(conv_float, axis=0)), "seq"
    )
    branch_grads = jnp.stack([grad_inner, grad_gate], axis=1)
    tok_part = jnp.einsum("tpe,pde->dt", branch_grads, in_full, preferred_element_type=jnp.float32)
    out_red = lax.psum_scatter(out_part, "dp", scatter_dimension=0, tiled=True)
    out_red = lax.optimization_barrier(out_red)
    output = out_red.T.astype(jnp.bfloat16)
    tok_split = tok_part.reshape(n_dp, tok_part.shape[0] // n_dp, tok_rows)
    tok_red = lax.all_to_all(tok_split, "dp", 0, 0, tiled=True).sum(axis=0)
    grad_tokens = tok_red.T.astype(jnp.bfloat16)
    term_in = jnp.einsum("td,tpe->pde", whole, branch_grads, preferred_element_type=jnp.float32)
    term_out_t = jnp.einsum("td,te->de", upstream, hidden, preferred_element_type=jnp.float32)
    terms = jnp.concatenate([term_in, term_out_t[None]], axis=0).astype(jnp.bfloat16)
    terms = terms.reshape(terms.shape[0], n_seq, terms.shape[1] // n_seq, terms.shape[2])
    terms = lax.all_to_all(terms, "seq", 1, 1, tiled=True).astype(jnp.float32).sum(axis=1)
    grad_in_weight = terms[:2]
    grad_out_weight = terms[2].T
    return (output, grad_tokens, grad_in_weight, grad_out_weight, tap_grads, bias_grads)


def solution(mesh):
    return jax.shard_map(
        on_device,
        mesh=mesh,
        in_specs=(
            P("seq", "dp"),
            P(None, "seq", "dp"),
            P(None, "dp"),
            P("dp"),
            P("dp", "seq"),
            P("seq", "dp"),
        ),
        out_specs=(
            P("seq", "dp"),
            P("seq", "dp"),
            P(None, "seq", "dp"),
            P("dp", "seq"),
            P(None, "dp"),
            P("dp"),
        ),
        check_vma=False,
    )
```

```python
import jax
import jax.numpy as jnp
from jax import lax
from jax.sharding import PartitionSpec as P


def from_behind(block, axis, distance):
    devices = range(lax.axis_size(axis))
    route = [(i - distance, i) for i in devices if i - distance in devices]
    return lax.ppermute(block, axis, route)


def silu_parts(value):
    sig = jax.nn.sigmoid(value)
    return (value * sig, sig * (1.0 + value * (1.0 - sig)))


def reduce_over_dp(part, n_dp):
    split = part.astype(jnp.bfloat16).reshape(n_dp, part.shape[0] // n_dp, part.shape[1])
    summed = lax.all_to_all(split, "dp", 0, 0, tiled=True).astype(jnp.float32).sum(axis=0)
    return summed.T.astype(jnp.bfloat16)


def on_device(tokens, in_weight, conv_weight, conv_bias, out_weight, grad_out):
    n_seq = lax.axis_size("seq")
    n_dp = lax.axis_size("dp")
    w_local = jnp.concatenate([in_weight, out_weight.T[None]], axis=0)
    w_rep = jnp.broadcast_to(w_local[None], (n_seq,) + w_local.shape)
    w_full = lax.all_to_all(w_rep, "seq", 0, 2, tiled=True)[0]
    in_full = w_full[:2]
    out_full_t = w_full[2]
    acts = jnp.stack([tokens, grad_out], axis=1)
    acts_full = lax.all_gather(acts, "dp", axis=2, tiled=True)
    whole = acts_full[:, 0]
    upstream = acts_full[:, 1]
    tok_rows = whole.shape[0]
    taps = conv_weight.shape[0]
    mixed = jnp.einsum("td,pde->tpe", whole, in_full, preferred_element_type=jnp.float32).astype(
        jnp.bfloat16
    )
    inner = mixed[:, 0, :]
    gate_in = mixed[:, 1, :]
    rim = from_behind(inner[tok_rows - (taps - 1) :], "seq", 1)
    padded = jnp.concatenate([rim, inner], axis=0)
    conv = jnp.broadcast_to(conv_bias.astype(jnp.float32)[None, :], inner.shape)
    for lag in range(taps):
        conv = conv + conv_weight[lag].astype(jnp.float32)[None, :] * padded[
            lag : lag + tok_rows
        ].astype(jnp.float32)
    act, act_slope = silu_parts(conv)
    gate, gate_slope = silu_parts(gate_in.astype(jnp.float32))
    hidden = (act * gate).astype(jnp.bfloat16)
    out_part = jnp.einsum("te,de->dt", hidden, out_full_t, preferred_element_type=jnp.float32)
    back = jnp.einsum("td,de->te", upstream, out_full_t, preferred_element_type=jnp.float32)
    grad_conv = (back * gate * act_slope).astype(jnp.bfloat16)
    grad_gate = (back * act * gate_slope).astype(jnp.bfloat16)
    ahead_rim = from_behind(grad_conv[: taps - 1], "seq", -1)
    ahead = jnp.concatenate([grad_conv, ahead_rim], axis=0)
    grad_inner = jnp.zeros(inner.shape, jnp.float32)
    for lag in range(taps):
        shift_start = taps - 1 - lag
        grad_inner = grad_inner + conv_weight[lag].astype(jnp.float32)[None, :] * ahead[
            shift_start : shift_start + tok_rows
        ].astype(jnp.float32)
    grad_inner = grad_inner.astype(jnp.bfloat16)
    conv_float = grad_conv.astype(jnp.float32)
    tap_rows = []
    for lag in range(taps):
        tap_rows.append(
            jnp.sum(conv_float * padded[lag : lag + tok_rows].astype(jnp.float32), axis=0)
        )
    conv_grads = jnp.concatenate([jnp.stack(tap_rows, axis=0), jnp.sum(conv_float, axis=0)[None]], axis=0)
    conv_grads = lax.all_gather(conv_grads, "seq", axis=0, tiled=False).sum(axis=0)
    tap_grads = conv_grads[:taps]
    bias_grads = conv_grads[taps]
    branch_grads = jnp.stack([grad_inner, grad_gate], axis=1)
    tok_part = jnp.einsum("tpe,pde->dt", branch_grads, in_full, preferred_element_type=jnp.float32)
    output = reduce_over_dp(out_part, n_dp)
    grad_tokens = reduce_over_dp(tok_part, n_dp)
    term_in = jnp.einsum("td,tpe->pde", whole, branch_grads, preferred_element_type=jnp.float32)
    term_out_t = jnp.einsum("td,te->de", upstream, hidden, preferred_element_type=jnp.float32)
    terms = jnp.concatenate([term_in, term_out_t[None]], axis=0).astype(jnp.bfloat16)
    terms = terms.reshape(terms.shape[0], n_seq, terms.shape[1] // n_seq, terms.shape[2])
    terms = lax.all_to_all(terms, "seq", 1, 1, tiled=True).astype(jnp.float32).sum(axis=1)
    grad_in_weight = terms[:2]
    grad_out_weight = terms[2].T
    return (output, grad_tokens, grad_in_weight, grad_out_weight, tap_grads, bias_grads)


def solution(mesh):
    return jax.shard_map(
        on_device,
        mesh=mesh,
        in_specs=(
            P("seq", "dp"),
            P(None, "seq", "dp"),
            P(None, "dp"),
            P("dp"),
            P("dp", "seq"),
            P("seq", "dp"),
        ),
        out_specs=(
            P("seq", "dp"),
            P("seq", "dp"),
            P(None, "seq", "dp"),
            P("dp", "seq"),
            P(None, "dp"),
            P("dp"),
        ),
        check_vma=False,
    )
```

```python
import jax
import jax.numpy as jnp
from jax import lax
from jax.sharding import PartitionSpec as P


def from_behind(block, axis, distance):
    devices = range(lax.axis_size(axis))
    route = [(i - distance, i) for i in devices if i - distance in devices]
    return lax.ppermute(block, axis, route)


def silu_parts(value):
    sig = jax.nn.sigmoid(value)
    return (value * sig, sig * (1.0 + value * (1.0 - sig)))


def gather_over(block, axis, n):
    rep = jnp.broadcast_to(block[None], (n,) + block.shape)
    return lax.all_to_all(rep, axis, 0, 2, tiled=True)[0]


def split_exact(value):
    hi = value.astype(jnp.bfloat16)
    rest = value - hi.astype(jnp.float32)
    mid = rest.astype(jnp.bfloat16)
    lo = (rest - mid.astype(jnp.float32)).astype(jnp.bfloat16)
    return jnp.concatenate([hi, mid, lo], axis=0)


def reduce_over_dp(part, n_dp):
    split = part.astype(jnp.bfloat16).reshape(n_dp, part.shape[0] // n_dp, part.shape[1])
    summed = lax.all_to_all(split, "dp", 0, 0, tiled=True).astype(jnp.float32).sum(axis=0)
    return summed.T.astype(jnp.bfloat16)


def on_device(tokens, in_weight, conv_weight, conv_bias, out_weight, grad_out):
    n_seq = lax.axis_size("seq")
    n_dp = lax.axis_size("dp")
    w_local = jnp.concatenate([in_weight, out_weight.T[None]], axis=0)
    w_full = gather_over(w_local, "seq", n_seq)
    in_full = w_full[:2]
    out_full_t = w_full[2]
    whole = gather_over(tokens, "dp", n_dp)
    upstream = gather_over(grad_out, "dp", n_dp)
    tok_rows = whole.shape[0]
    taps = conv_weight.shape[0]
    mixed = jnp.einsum("td,pde->tpe", whole, in_full, preferred_element_type=jnp.float32).astype(
        jnp.bfloat16
    )
    inner = mixed[:, 0, :]
    gate_in = mixed[:, 1, :]
    rim = from_behind(inner[tok_rows - (taps - 1) :], "seq", 1)
    padded = jnp.concatenate([rim, inner], axis=0)
    conv = jnp.broadcast_to(conv_bias.astype(jnp.float32)[None, :], inner.shape)
    for lag in range(taps):
        conv = conv + conv_weight[lag].astype(jnp.float32)[None, :] * padded[
            lag : lag + tok_rows
        ].astype(jnp.float32)
    act, act_slope = silu_parts(conv)
    gate, gate_slope = silu_parts(gate_in.astype(jnp.float32))
    hidden = (act * gate).astype(jnp.bfloat16)
    out_part = jnp.einsum("te,de->dt", hidden, out_full_t, preferred_element_type=jnp.float32)
    back = jnp.einsum("td,de->te", upstream, out_full_t, preferred_element_type=jnp.float32)
    grad_conv = (back * gate * act_slope).astype(jnp.bfloat16)
    grad_gate = (back * act * gate_slope).astype(jnp.bfloat16)
    ahead_rim = from_behind(grad_conv[: taps - 1], "seq", -1)
    ahead = jnp.concatenate([grad_conv, ahead_rim], axis=0)
    grad_inner = jnp.zeros(inner.shape, jnp.float32)
    for lag in range(taps):
        shift_start = taps - 1 - lag
        grad_inner = grad_inner + conv_weight[lag].astype(jnp.float32)[None, :] * ahead[
            shift_start : shift_start + tok_rows
        ].astype(jnp.float32)
    grad_inner = grad_inner.astype(jnp.bfloat16)
    conv_float = grad_conv.astype(jnp.float32)
    tap_rows = []
    for lag in range(taps):
        tap_rows.append(
            jnp.sum(conv_float * padded[lag : lag + tok_rows].astype(jnp.float32), axis=0)
        )
    conv_grads = jnp.concatenate([jnp.stack(tap_rows, axis=0), jnp.sum(conv_float, axis=0)[None]], axis=0)
    branch_grads = jnp.stack([grad_inner, grad_gate], axis=1)
    tok_part = jnp.einsum("tpe,pde->dt", branch_grads, in_full, preferred_element_type=jnp.float32)
    output = reduce_over_dp(out_part, n_dp)
    grad_tokens = reduce_over_dp(tok_part, n_dp)
    term_in = jnp.einsum("td,tpe->pde", whole, branch_grads, preferred_element_type=jnp.float32)
    term_out_t = jnp.einsum("td,te->de", upstream, hidden, preferred_element_type=jnp.float32)
    terms = jnp.concatenate([term_in, term_out_t[None]], axis=0).astype(jnp.bfloat16)
    n_mats, d_full, e_loc = terms.shape
    d_loc = d_full // n_seq
    terms = terms.reshape(n_mats, n_seq, d_loc, e_loc).transpose(1, 0, 2, 3)
    terms = terms.reshape(n_seq, n_mats * d_loc, e_loc)
    conv_parts = split_exact(conv_grads)
    n_conv = conv_parts.shape[0]
    pad_rows = (-n_conv) % 8
    conv_parts = jnp.concatenate([conv_parts, jnp.zeros((pad_rows, e_loc), jnp.bfloat16)], axis=0)
    conv_parts = jnp.broadcast_to(conv_parts[None], (n_seq,) + conv_parts.shape)
    sent = jnp.concatenate([terms, conv_parts], axis=1)
    summed = lax.all_to_all(sent, "seq", 0, 0, tiled=True).astype(jnp.float32).sum(axis=0)
    weights = summed[: n_mats * d_loc].reshape(n_mats, d_loc, e_loc)
    grad_in_weight = weights[:2]
    grad_out_weight = weights[2].T
    conv_sum = summed[n_mats * d_loc : n_mats * d_loc + n_conv]
    n_row = taps + 1
    conv_sum = (conv_sum[:n_row] + conv_sum[n_row : 2 * n_row]) + conv_sum[2 * n_row :]
    tap_grads = conv_sum[:taps]
    bias_grads = conv_sum[taps]
    return (output, grad_tokens, grad_in_weight, grad_out_weight, tap_grads, bias_grads)


def solution(mesh):
    return jax.shard_map(
        on_device,
        mesh=mesh,
        in_specs=(
            P("seq", "dp"),
            P(None, "seq", "dp"),
            P(None, "dp"),
            P("dp"),
            P("dp", "seq"),
            P("seq", "dp"),
        ),
        out_specs=(
            P("seq", "dp"),
            P("seq", "dp"),
            P(None, "seq", "dp"),
            P("dp", "seq"),
            P(None, "dp"),
            P("dp"),
        ),
        check_vma=False,
    )
```

```python
import jax
import jax.numpy as jnp
from jax import lax
from jax.sharding import PartitionSpec as P


def from_behind(block, axis, distance):
    devices = range(lax.axis_size(axis))
    route = [(i - distance, i) for i in devices if i - distance in devices]
    return lax.ppermute(block, axis, route)


def silu_parts(value):
    sig = jax.nn.sigmoid(value)
    return (value * sig, sig * (1.0 + value * (1.0 - sig)))


def gather_over(block, axis, n):
    rep = jnp.broadcast_to(block[None], (n,) + block.shape)
    return lax.all_to_all(rep, axis, 0, 2, tiled=True)[0]


def split_exact(value):
    hi = value.astype(jnp.bfloat16)
    rest = value - hi.astype(jnp.float32)
    mid = rest.astype(jnp.bfloat16)
    lo = (rest - mid.astype(jnp.float32)).astype(jnp.bfloat16)
    return jnp.concatenate([hi, mid, lo], axis=0)


def reduce_over_dp(part, n_dp):
    split = part.astype(jnp.bfloat16).reshape(n_dp, part.shape[0] // n_dp, part.shape[1])
    summed = lax.all_to_all(split, "dp", 0, 0, tiled=True).astype(jnp.float32).sum(axis=0)
    return summed.T.astype(jnp.bfloat16)


def on_device(tokens, in_weight, conv_weight, conv_bias, out_weight, grad_out):
    n_seq = lax.axis_size("seq")
    n_dp = lax.axis_size("dp")
    w_local = jnp.concatenate([in_weight, out_weight.T[None]], axis=0)
    w_full = lax.all_gather(w_local, "seq", axis=1, tiled=True)
    in_full = w_full[:2]
    out_full_t = w_full[2]
    whole = gather_over(tokens, "dp", n_dp)
    upstream = gather_over(grad_out, "dp", n_dp)
    tok_rows = whole.shape[0]
    taps = conv_weight.shape[0]
    mixed = jnp.einsum("td,pde->tpe", whole, in_full, preferred_element_type=jnp.float32).astype(
        jnp.bfloat16
    )
    inner = mixed[:, 0, :]
    gate_in = mixed[:, 1, :]
    rim = from_behind(inner[tok_rows - (taps - 1) :], "seq", 1)
    padded = jnp.concatenate([rim, inner], axis=0)
    conv = jnp.broadcast_to(conv_bias.astype(jnp.float32)[None, :], inner.shape)
    for lag in range(taps):
        conv = conv + conv_weight[lag].astype(jnp.float32)[None, :] * padded[
            lag : lag + tok_rows
        ].astype(jnp.float32)
    act, act_slope = silu_parts(conv)
    gate, gate_slope = silu_parts(gate_in.astype(jnp.float32))
    hidden = (act * gate).astype(jnp.bfloat16)
    out_part = jnp.einsum("te,de->dt", hidden, out_full_t, preferred_element_type=jnp.float32)
    back = jnp.einsum("td,de->te", upstream, out_full_t, preferred_element_type=jnp.float32)
    grad_conv = (back * gate * act_slope).astype(jnp.bfloat16)
    grad_gate = (back * act * gate_slope).astype(jnp.bfloat16)
    ahead_rim = from_behind(grad_conv[: taps - 1], "seq", -1)
    ahead = jnp.concatenate([grad_conv, ahead_rim], axis=0)
    grad_inner = jnp.zeros(inner.shape, jnp.float32)
    for lag in range(taps):
        shift_start = taps - 1 - lag
        grad_inner = grad_inner + conv_weight[lag].astype(jnp.float32)[None, :] * ahead[
            shift_start : shift_start + tok_rows
        ].astype(jnp.float32)
    grad_inner = grad_inner.astype(jnp.bfloat16)
    conv_float = grad_conv.astype(jnp.float32)
    tap_rows = []
    for lag in range(taps):
        tap_rows.append(
            jnp.sum(conv_float * padded[lag : lag + tok_rows].astype(jnp.float32), axis=0)
        )
    conv_grads = jnp.concatenate([jnp.stack(tap_rows, axis=0), jnp.sum(conv_float, axis=0)[None]], axis=0)
    branch_grads = jnp.stack([grad_inner, grad_gate], axis=1)
    tok_part = jnp.einsum("tpe,pde->dt", branch_grads, in_full, preferred_element_type=jnp.float32)
    output = reduce_over_dp(out_part, n_dp)
    grad_tokens = reduce_over_dp(tok_part, n_dp)
    term_in = jnp.einsum("td,tpe->pde", whole, branch_grads, preferred_element_type=jnp.float32)
    term_out_t = jnp.einsum("td,te->de", upstream, hidden, preferred_element_type=jnp.float32)
    terms = jnp.concatenate([term_in, term_out_t[None]], axis=0).astype(jnp.bfloat16)
    terms = lax.psum_scatter(terms, "seq", scatter_dimension=1, tiled=True).astype(jnp.float32)
    grad_in_weight = terms[:2]
    grad_out_weight = terms[2].T
    n_row = taps + 1
    shift = 1
    while shift < n_seq:
        parts = lax.ppermute(
            split_exact(conv_grads), "seq", [(i, (i + shift) % n_seq) for i in range(n_seq)]
        ).astype(jnp.float32)
        conv_grads = conv_grads + ((parts[:n_row] + parts[n_row : 2 * n_row]) + parts[2 * n_row :])
        shift *= 2
    tap_grads = conv_grads[:taps]
    bias_grads = conv_grads[taps]
    return (output, grad_tokens, grad_in_weight, grad_out_weight, tap_grads, bias_grads)


def solution(mesh):
    return jax.shard_map(
        on_device,
        mesh=mesh,
        in_specs=(
            P("seq", "dp"),
            P(None, "seq", "dp"),
            P(None, "dp"),
            P("dp"),
            P("dp", "seq"),
            P("seq", "dp"),
        ),
        out_specs=(
            P("seq", "dp"),
            P("seq", "dp"),
            P(None, "seq", "dp"),
            P("dp", "seq"),
            P(None, "dp"),
            P("dp"),
        ),
        check_vma=False,
    )
```

```python
import jax
import jax.numpy as jnp
from jax import lax
from jax.sharding import PartitionSpec as P


def from_behind(block, axis, distance):
    devices = range(lax.axis_size(axis))
    route = [(i - distance, i) for i in devices if i - distance in devices]
    return lax.ppermute(block, axis, route)


def silu_parts(value):
    sig = jax.nn.sigmoid(value)
    return (value * sig, sig * (1.0 + value * (1.0 - sig)))


def gather_over(block, axis, n, dim):
    rep = jnp.broadcast_to(block[None], (n,) + block.shape)
    return lax.all_to_all(rep, axis, 0, dim + 1, tiled=True)[0]


def split_exact(value):
    hi = value.astype(jnp.bfloat16)
    rest = value - hi.astype(jnp.float32)
    mid = rest.astype(jnp.bfloat16)
    lo = (rest - mid.astype(jnp.float32)).astype(jnp.bfloat16)
    return jnp.concatenate([hi, mid, lo], axis=0)


def reduce_over_dp(part, n_dp):
    split = part.astype(jnp.bfloat16).reshape((n_dp, part.shape[0] // n_dp) + part.shape[1:])
    return lax.all_to_all(split, "dp", 0, 0, tiled=True).astype(jnp.float32).sum(axis=0)


def on_device(tokens, in_weight, conv_weight, conv_bias, out_weight, grad_out):
    n_seq = lax.axis_size("seq")
    n_dp = lax.axis_size("dp")
    w_local = jnp.concatenate([in_weight, out_weight.T[None]], axis=0)
    w_full = lax.all_gather(w_local, "seq", axis=1, tiled=True)
    in_full = w_full[:2]
    out_full_t = w_full[2]
    acts = gather_over(jnp.stack([tokens, grad_out], axis=1), "dp", n_dp, 2)
    whole = acts[:, 0]
    upstream = acts[:, 1]
    tok_rows = whole.shape[0]
    taps = conv_weight.shape[0]
    mixed = jnp.einsum("td,pde->tpe", whole, in_full, preferred_element_type=jnp.float32).astype(
        jnp.bfloat16
    )
    inner = mixed[:, 0, :]
    gate_in = mixed[:, 1, :]
    rim = from_behind(inner[tok_rows - (taps - 1) :], "seq", 1)
    padded = jnp.concatenate([rim, inner], axis=0)
    conv = jnp.broadcast_to(conv_bias.astype(jnp.float32)[None, :], inner.shape)
    for lag in range(taps):
        conv = conv + conv_weight[lag].astype(jnp.float32)[None, :] * padded[
            lag : lag + tok_rows
        ].astype(jnp.float32)
    act, act_slope = silu_parts(conv)
    gate, gate_slope = silu_parts(gate_in.astype(jnp.float32))
    hidden = (act * gate).astype(jnp.bfloat16)
    out_part = jnp.einsum("te,de->dt", hidden, out_full_t, preferred_element_type=jnp.float32)
    back = jnp.einsum("td,de->te", upstream, out_full_t, preferred_element_type=jnp.float32)
    grad_conv = (back * gate * act_slope).astype(jnp.bfloat16)
    grad_gate = (back * act * gate_slope).astype(jnp.bfloat16)
    ahead_rim = from_behind(grad_conv[: taps - 1], "seq", -1)
    ahead = jnp.concatenate([grad_conv, ahead_rim], axis=0)
    grad_inner = jnp.zeros(inner.shape, jnp.float32)
    for lag in range(taps):
        shift_start = taps - 1 - lag
        grad_inner = grad_inner + conv_weight[lag].astype(jnp.float32)[None, :] * ahead[
            shift_start : shift_start + tok_rows
        ].astype(jnp.float32)
    grad_inner = grad_inner.astype(jnp.bfloat16)
    conv_float = grad_conv.astype(jnp.float32)
    tap_rows = []
    for lag in range(taps):
        tap_rows.append(
            jnp.sum(conv_float * padded[lag : lag + tok_rows].astype(jnp.float32), axis=0)
        )
    conv_grads = jnp.concatenate([jnp.stack(tap_rows, axis=0), jnp.sum(conv_float, axis=0)[None]], axis=0)
    branch_grads = jnp.stack([grad_inner, grad_gate], axis=1)
    tok_part = jnp.einsum("tpe,pde->dt", branch_grads, in_full, preferred_element_type=jnp.float32)
    reduced = reduce_over_dp(jnp.stack([out_part, tok_part], axis=1), n_dp)
    output = reduced[:, 0].T.astype(jnp.bfloat16)
    grad_tokens = reduced[:, 1].T.astype(jnp.bfloat16)
    term_in = jnp.einsum("td,tpe->pde", whole, branch_grads, preferred_element_type=jnp.float32)
    term_out_t = jnp.einsum("td,te->de", upstream, hidden, preferred_element_type=jnp.float32)
    terms = jnp.concatenate([term_in, term_out_t[None]], axis=0).astype(jnp.bfloat16)
    terms = lax.psum_scatter(terms, "seq", scatter_dimension=1, tiled=True).astype(jnp.float32)
    grad_in_weight = terms[:2]
    grad_out_weight = terms[2].T
    n_row = taps + 1
    shift = 1
    while shift < n_seq:
        parts = lax.ppermute(
            split_exact(conv_grads), "seq", [(i, (i + shift) % n_seq) for i in range(n_seq)]
        ).astype(jnp.float32)
        conv_grads = conv_grads + ((parts[:n_row] + parts[n_row : 2 * n_row]) + parts[2 * n_row :])
        shift *= 2
    tap_grads = conv_grads[:taps]
    bias_grads = conv_grads[taps]
    return (output, grad_tokens, grad_in_weight, grad_out_weight, tap_grads, bias_grads)


def solution(mesh):
    return jax.shard_map(
        on_device,
        mesh=mesh,
        in_specs=(
            P("seq", "dp"),
            P(None, "seq", "dp"),
            P(None, "dp"),
            P("dp"),
            P("dp", "seq"),
            P("seq", "dp"),
        ),
        out_specs=(
            P("seq", "dp"),
            P("seq", "dp"),
            P(None, "seq", "dp"),
            P("dp", "seq"),
            P(None, "dp"),
            P("dp"),
        ),
        check_vma=False,
    )
```

```python
import jax
import jax.numpy as jnp
from jax import lax
from jax.sharding import PartitionSpec as P


DP = ("chip", "core")


def from_behind(block, axis, distance):
    devices = range(lax.axis_size(axis))
    route = [(i - distance, i) for i in devices if i - distance in devices]
    return lax.ppermute(block, axis, route)


def silu_parts(value):
    sig = jax.nn.sigmoid(value)
    return (value * sig, sig * (1.0 + value * (1.0 - sig)))


def gather_over(block, axis, n, dim):
    rep = jnp.broadcast_to(block[None], (n,) + block.shape)
    return lax.all_to_all(rep, axis, 0, dim + 1, tiled=True)[0]


def split_exact(value):
    hi = value.astype(jnp.bfloat16)
    rest = value - hi.astype(jnp.float32)
    mid = rest.astype(jnp.bfloat16)
    lo = (rest - mid.astype(jnp.float32)).astype(jnp.bfloat16)
    return jnp.concatenate([hi, mid, lo], axis=0)


def reduce_over_dp(part, n_chip, n_core):
    split = part.reshape((n_chip, n_core, part.shape[0] // (n_chip * n_core)) + part.shape[1:])
    split = lax.all_to_all(split, "core", 1, 1, tiled=True).sum(axis=1)
    split = split.astype(jnp.bfloat16)
    return lax.all_to_all(split, "chip", 0, 0, tiled=True).astype(jnp.float32).sum(axis=0)


def on_device(tokens, in_weight, conv_weight, conv_bias, out_weight, grad_out):
    n_seq = lax.axis_size("seq")
    n_chip = lax.axis_size("chip")
    n_core = lax.axis_size("core")
    n_dp = n_chip * n_core
    w_local = jnp.concatenate([in_weight, out_weight.T[None]], axis=0)
    w_full = lax.all_gather(w_local, "seq", axis=1, tiled=True)
    in_full = w_full[:2]
    out_full_t = w_full[2]
    acts = gather_over(jnp.stack([tokens, grad_out], axis=1), "chip", n_chip, 2)
    acts = gather_over(acts.reshape(acts.shape[:2] + (n_chip, 1, -1)), "core", n_core, 3)
    acts = acts.reshape(acts.shape[:2] + (-1,))
    whole = acts[:, 0]
    upstream = acts[:, 1]
    tok_rows = whole.shape[0]
    taps = conv_weight.shape[0]
    mixed = jnp.einsum("td,pde->tpe", whole, in_full, preferred_element_type=jnp.float32).astype(
        jnp.bfloat16
    )
    inner = mixed[:, 0, :]
    gate_in = mixed[:, 1, :]
    rim = from_behind(inner[tok_rows - (taps - 1) :], "seq", 1)
    padded = jnp.concatenate([rim, inner], axis=0)
    conv = jnp.broadcast_to(conv_bias.astype(jnp.float32)[None, :], inner.shape)
    for lag in range(taps):
        conv = conv + conv_weight[lag].astype(jnp.float32)[None, :] * padded[
            lag : lag + tok_rows
        ].astype(jnp.float32)
    act, act_slope = silu_parts(conv)
    gate, gate_slope = silu_parts(gate_in.astype(jnp.float32))
    hidden = (act * gate).astype(jnp.bfloat16)
    out_part = jnp.einsum("te,de->dt", hidden, out_full_t, preferred_element_type=jnp.float32)
    back = jnp.einsum("td,de->te", upstream, out_full_t, preferred_element_type=jnp.float32)
    grad_conv = (back * gate * act_slope).astype(jnp.bfloat16)
    grad_gate = (back * act * gate_slope).astype(jnp.bfloat16)
    ahead_rim = from_behind(grad_conv[: taps - 1], "seq", -1)
    ahead = jnp.concatenate([grad_conv, ahead_rim], axis=0)
    grad_inner = jnp.zeros(inner.shape, jnp.float32)
    for lag in range(taps):
        shift_start = taps - 1 - lag
        grad_inner = grad_inner + conv_weight[lag].astype(jnp.float32)[None, :] * ahead[
            shift_start : shift_start + tok_rows
        ].astype(jnp.float32)
    grad_inner = grad_inner.astype(jnp.bfloat16)
    conv_float = grad_conv.astype(jnp.float32)
    tap_rows = []
    for lag in range(taps):
        tap_rows.append(
            jnp.sum(conv_float * padded[lag : lag + tok_rows].astype(jnp.float32), axis=0)
        )
    conv_grads = jnp.concatenate([jnp.stack(tap_rows, axis=0), jnp.sum(conv_float, axis=0)[None]], axis=0)
    branch_grads = jnp.stack([grad_inner, grad_gate], axis=1)
    tok_part = jnp.einsum("tpe,pde->dt", branch_grads, in_full, preferred_element_type=jnp.float32)
    reduced = reduce_over_dp(jnp.stack([out_part, tok_part], axis=1), n_chip, n_core)
    output = reduced[:, 0].T.astype(jnp.bfloat16)
    grad_tokens = reduced[:, 1].T.astype(jnp.bfloat16)
    term_in = jnp.einsum("td,tpe->pde", whole, branch_grads, preferred_element_type=jnp.float32)
    term_out_t = jnp.einsum("td,te->de", upstream, hidden, preferred_element_type=jnp.float32)
    terms = jnp.concatenate([term_in, term_out_t[None]], axis=0).astype(jnp.bfloat16)
    terms = lax.psum_scatter(terms, "seq", scatter_dimension=1, tiled=True).astype(jnp.float32)
    grad_in_weight = terms[:2]
    grad_out_weight = terms[2].T
    n_row = taps + 1
    shift = 1
    while shift < n_seq:
        parts = lax.ppermute(
            split_exact(conv_grads), "seq", [(i, (i + shift) % n_seq) for i in range(n_seq)]
        ).astype(jnp.float32)
        conv_grads = conv_grads + ((parts[:n_row] + parts[n_row : 2 * n_row]) + parts[2 * n_row :])
        shift *= 2
    tap_grads = conv_grads[:taps]
    bias_grads = conv_grads[taps]
    return (output, grad_tokens, grad_in_weight, grad_out_weight, tap_grads, bias_grads)


def solution(mesh):
    n_core = 2
    devices = mesh.devices.reshape(mesh.devices.shape[0] // n_core, n_core, mesh.devices.shape[1])
    split_mesh = jax.sharding.Mesh(devices, ("chip", "core", "seq"))
    return jax.shard_map(
        on_device,
        mesh=split_mesh,
        in_specs=(
            P("seq", DP),
            P(None, "seq", DP),
            P(None, DP),
            P(DP),
            P(DP, "seq"),
            P("seq", DP),
        ),
        out_specs=(
            P("seq", DP),
            P("seq", DP),
            P(None, "seq", DP),
            P(DP, "seq"),
            P(None, DP),
            P(DP),
        ),
        check_vma=False,
    )
```

```python
import jax
import jax.numpy as jnp
from jax import lax
from jax.sharding import PartitionSpec as P


DP = ("chip", "core")


def from_behind(block, axis, distance):
    devices = range(lax.axis_size(axis))
    route = [(i - distance, i) for i in devices if i - distance in devices]
    return lax.ppermute(block, axis, route)


def silu_parts(value):
    sig = jax.nn.sigmoid(value)
    return (value * sig, sig * (1.0 + value * (1.0 - sig)))


def gather_over(block, axis, n, dim):
    rep = jnp.broadcast_to(block[None], (n,) + block.shape)
    return lax.all_to_all(rep, axis, 0, dim + 1, tiled=True)[0]


def split_exact(value):
    hi = value.astype(jnp.bfloat16)
    rest = value - hi.astype(jnp.float32)
    mid = rest.astype(jnp.bfloat16)
    lo = (rest - mid.astype(jnp.float32)).astype(jnp.bfloat16)
    return jnp.concatenate([hi, mid, lo], axis=0)


def reduce_over_dp(part, n_chip, n_core):
    split = part.reshape((n_chip, n_core, part.shape[0] // (n_chip * n_core)) + part.shape[1:])
    split = lax.all_to_all(split, "core", 1, 1, tiled=True).sum(axis=1)
    split = split.astype(jnp.bfloat16)
    return lax.all_to_all(split, "chip", 0, 0, tiled=True).astype(jnp.float32).sum(axis=0)


def on_device(tokens, in_weight, conv_weight, conv_bias, out_weight, grad_out):
    n_seq = lax.axis_size("seq")
    n_chip = lax.axis_size("chip")
    n_core = lax.axis_size("core")
    n_dp = n_chip * n_core
    w_local = jnp.concatenate([in_weight, out_weight.T[None]], axis=0)
    w_full = lax.all_gather(w_local, "seq", axis=1, tiled=True)
    in_full = w_full[:2]
    out_full_t = w_full[2]
    acts = gather_over(jnp.stack([tokens, grad_out], axis=1), "chip", n_chip, 2)
    acts = gather_over(acts.reshape(acts.shape[:2] + (n_chip, 1, -1)), "core", n_core, 3)
    acts = acts.reshape(acts.shape[:2] + (-1,))
    whole = acts[:, 0]
    upstream = acts[:, 1]
    tok_rows = whole.shape[0]
    taps = conv_weight.shape[0]
    mixed = jnp.einsum("td,pde->tpe", whole, in_full, preferred_element_type=jnp.float32).astype(
        jnp.bfloat16
    )
    inner = mixed[:, 0, :]
    gate_in = mixed[:, 1, :]
    rim = from_behind(inner[tok_rows - (taps - 1) :], "seq", 1)
    padded = jnp.concatenate([rim, inner], axis=0)
    conv = jnp.broadcast_to(conv_bias.astype(jnp.float32)[None, :], inner.shape)
    for lag in range(taps):
        conv = conv + conv_weight[lag].astype(jnp.float32)[None, :] * padded[
            lag : lag + tok_rows
        ].astype(jnp.float32)
    act, act_slope = silu_parts(conv)
    gate, gate_slope = silu_parts(gate_in.astype(jnp.float32))
    hidden = (act * gate).astype(jnp.bfloat16)
    out_part = jnp.einsum("te,de->dt", hidden, out_full_t, preferred_element_type=jnp.float32)
    back = jnp.einsum("td,de->te", upstream, out_full_t, preferred_element_type=jnp.float32)
    grad_conv = (back * gate * act_slope).astype(jnp.bfloat16)
    grad_gate = (back * act * gate_slope).astype(jnp.bfloat16)
    ahead_rim = from_behind(grad_conv[: taps - 1], "seq", -1)
    ahead = jnp.concatenate([grad_conv, ahead_rim], axis=0)
    grad_inner = jnp.zeros(inner.shape, jnp.float32)
    for lag in range(taps):
        shift_start = taps - 1 - lag
        grad_inner = grad_inner + conv_weight[lag].astype(jnp.float32)[None, :] * ahead[
            shift_start : shift_start + tok_rows
        ].astype(jnp.float32)
    grad_inner = grad_inner.astype(jnp.bfloat16)
    conv_float = grad_conv.astype(jnp.float32)
    tap_rows = []
    for lag in range(taps):
        tap_rows.append(
            jnp.sum(conv_float * padded[lag : lag + tok_rows].astype(jnp.float32), axis=0)
        )
    conv_grads = jnp.concatenate([jnp.stack(tap_rows, axis=0), jnp.sum(conv_float, axis=0)[None]], axis=0)
    branch_grads = jnp.stack([grad_inner, grad_gate], axis=1)
    tok_part = jnp.einsum("tpe,pde->dt", branch_grads, in_full, preferred_element_type=jnp.float32)
    reduced = reduce_over_dp(jnp.stack([out_part, tok_part], axis=1), n_chip, n_core)
    output = reduced[:, 0].T.astype(jnp.bfloat16)
    grad_tokens = reduced[:, 1].T.astype(jnp.bfloat16)
    term_in = jnp.einsum("td,tpe->pde", whole, branch_grads, preferred_element_type=jnp.float32)
    term_out_t = jnp.einsum("td,te->de", upstream, hidden, preferred_element_type=jnp.float32)
    grad_in_weight = lax.psum_scatter(
        term_in.astype(jnp.bfloat16), "seq", scatter_dimension=1, tiled=True
    ).astype(jnp.float32)
    d_full, e_loc = term_out_t.shape
    d_loc = d_full // n_seq
    sent = term_out_t.astype(jnp.bfloat16).reshape(n_seq, d_loc, e_loc)
    conv_parts = split_exact(conv_grads)
    n_conv = conv_parts.shape[0]
    pad_rows = (-n_conv) % 8
    conv_parts = jnp.concatenate([conv_parts, jnp.zeros((pad_rows, e_loc), jnp.bfloat16)], axis=0)
    conv_parts = jnp.broadcast_to(conv_parts[None], (n_seq,) + conv_parts.shape)
    sent = jnp.concatenate([sent, conv_parts], axis=1)
    summed = lax.all_to_all(sent, "seq", 0, 0, tiled=True).astype(jnp.float32).sum(axis=0)
    grad_out_weight = summed[:d_loc].T
    conv_sum = summed[d_loc : d_loc + n_conv]
    n_row = taps + 1
    conv_sum = (conv_sum[:n_row] + conv_sum[n_row : 2 * n_row]) + conv_sum[2 * n_row :]
    tap_grads = conv_sum[:taps]
    bias_grads = conv_sum[taps]
    return (output, grad_tokens, grad_in_weight, grad_out_weight, tap_grads, bias_grads)


def solution(mesh):
    n_core = 2
    devices = mesh.devices.reshape(mesh.devices.shape[0] // n_core, n_core, mesh.devices.shape[1])
    split_mesh = jax.sharding.Mesh(devices, ("chip", "core", "seq"))
    return jax.shard_map(
        on_device,
        mesh=split_mesh,
        in_specs=(
            P("seq", DP),
            P(None, "seq", DP),
            P(None, DP),
            P(DP),
            P(DP, "seq"),
            P("seq", DP),
        ),
        out_specs=(
            P("seq", DP),
            P("seq", DP),
            P(None, "seq", DP),
            P(DP, "seq"),
            P(None, DP),
            P(DP),
        ),
        check_vma=False,
    )
```

```python
import jax
import jax.numpy as jnp
from jax import lax
from jax.sharding import PartitionSpec as P


DP = ("chip", "core")


def from_behind(block, axis, distance):
    devices = range(lax.axis_size(axis))
    route = [(i - distance, i) for i in devices if i - distance in devices]
    return lax.ppermute(block, axis, route)


def silu_parts(value):
    sig = jax.nn.sigmoid(value)
    return (value * sig, sig * (1.0 + value * (1.0 - sig)))


def gather_over(block, axis, n, dim):
    rep = jnp.broadcast_to(block[None], (n,) + block.shape)
    return lax.all_to_all(rep, axis, 0, dim + 1, tiled=True)[0]


def split_exact(value):
    hi = value.astype(jnp.bfloat16)
    rest = value - hi.astype(jnp.float32)
    mid = rest.astype(jnp.bfloat16)
    lo = (rest - mid.astype(jnp.float32)).astype(jnp.bfloat16)
    return jnp.concatenate([hi, mid, lo], axis=0)


def reduce_over_dp(part, n_chip, n_core):
    split = part.reshape((n_chip, n_core, part.shape[0] // (n_chip * n_core)) + part.shape[1:])
    split = lax.all_to_all(split, "core", 1, 1, tiled=True).sum(axis=1)
    split = split.astype(jnp.bfloat16)
    return lax.all_to_all(split, "chip", 0, 0, tiled=True).astype(jnp.float32).sum(axis=0)


def on_device(tokens, in_weight, conv_weight, conv_bias, out_weight, grad_out):
    n_seq = lax.axis_size("seq")
    n_chip = lax.axis_size("chip")
    n_core = lax.axis_size("core")
    n_dp = n_chip * n_core
    w_local = jnp.concatenate([in_weight, out_weight.T[None]], axis=0)
    w_full = lax.all_gather(w_local, "seq", axis=1, tiled=True)
    in_full = w_full[:2]
    out_full_t = w_full[2]
    acts = gather_over(jnp.stack([tokens, grad_out], axis=1), "chip", n_chip, 2)
    acts = gather_over(acts.reshape(acts.shape[:2] + (n_chip, 1, -1)), "core", n_core, 3)
    acts = acts.reshape(acts.shape[:2] + (-1,))
    whole = acts[:, 0]
    upstream = acts[:, 1]
    tok_rows = whole.shape[0]
    taps = conv_weight.shape[0]
    mixed = jnp.einsum("td,pde->tpe", whole, in_full, preferred_element_type=jnp.float32).astype(
        jnp.bfloat16
    )
    inner = mixed[:, 0, :]
    gate_in = mixed[:, 1, :]
    rim = from_behind(inner[tok_rows - (taps - 1) :], "seq", 1)
    padded = jnp.concatenate([rim, inner], axis=0)
    conv = jnp.broadcast_to(conv_bias.astype(jnp.float32)[None, :], inner.shape)
    for lag in range(taps):
        conv = conv + conv_weight[lag].astype(jnp.float32)[None, :] * padded[
            lag : lag + tok_rows
        ].astype(jnp.float32)
    act, act_slope = silu_parts(conv)
    gate, gate_slope = silu_parts(gate_in.astype(jnp.float32))
    hidden = (act * gate).astype(jnp.bfloat16)
    out_part = jnp.einsum("te,de->dt", hidden, out_full_t, preferred_element_type=jnp.float32)
    back = jnp.einsum("td,de->te", upstream, out_full_t, preferred_element_type=jnp.float32)
    grad_conv = (back * gate * act_slope).astype(jnp.bfloat16)
    grad_gate = (back * act * gate_slope).astype(jnp.bfloat16)
    ahead_rim = from_behind(grad_conv[: taps - 1], "seq", -1)
    ahead = jnp.concatenate([grad_conv, ahead_rim], axis=0)
    grad_inner = jnp.zeros(inner.shape, jnp.float32)
    for lag in range(taps):
        shift_start = taps - 1 - lag
        grad_inner = grad_inner + conv_weight[lag].astype(jnp.float32)[None, :] * ahead[
            shift_start : shift_start + tok_rows
        ].astype(jnp.float32)
    grad_inner = grad_inner.astype(jnp.bfloat16)
    conv_float = grad_conv.astype(jnp.float32)
    tap_rows = []
    for lag in range(taps):
        tap_rows.append(
            jnp.sum(conv_float * padded[lag : lag + tok_rows].astype(jnp.float32), axis=0)
        )
    conv_grads = jnp.concatenate([jnp.stack(tap_rows, axis=0), jnp.sum(conv_float, axis=0)[None]], axis=0)
    branch_grads = jnp.stack([grad_inner, grad_gate], axis=1)
    tok_part = jnp.einsum("tpe,pde->dt", branch_grads, in_full, preferred_element_type=jnp.float32)
    reduced = reduce_over_dp(jnp.stack([out_part, tok_part], axis=1), n_chip, n_core)
    output = reduced[:, 0].T.astype(jnp.bfloat16)
    grad_tokens = reduced[:, 1].T.astype(jnp.bfloat16)
    term_in = jnp.einsum("td,tpe->dpe", whole, branch_grads, preferred_element_type=jnp.float32)
    term_out_t = jnp.einsum("td,te->de", upstream, hidden, preferred_element_type=jnp.float32)
    d_full, e_loc = term_out_t.shape
    d_loc = d_full // n_seq
    half = e_loc // 2
    on_sc = jnp.concatenate(
        [term_in.reshape(d_full, 2 * e_loc), term_out_t[:, :half]], axis=1
    ).astype(jnp.bfloat16)
    on_sc = lax.psum_scatter(on_sc, "seq", scatter_dimension=0, tiled=True).astype(jnp.float32)
    grad_in_weight = on_sc[:, : 2 * e_loc].reshape(d_loc, 2, e_loc).transpose(1, 0, 2)
    sent = term_out_t[:, half:].astype(jnp.bfloat16).reshape(n_seq, d_loc, e_loc - half)
    conv_parts = split_exact(conv_grads)
    n_conv = conv_parts.shape[0]
    pad_rows = (-n_conv) % 8
    conv_parts = jnp.concatenate([conv_parts, jnp.zeros((pad_rows, e_loc), jnp.bfloat16)], axis=0)
    conv_parts = conv_parts.reshape(-1, e_loc - half)
    conv_parts = jnp.broadcast_to(conv_parts[None], (n_seq,) + conv_parts.shape)
    sent = jnp.concatenate([sent, conv_parts], axis=1)
    summed = lax.all_to_all(sent, "seq", 0, 0, tiled=True).astype(jnp.float32).sum(axis=0)
    grad_out_weight = jnp.concatenate([on_sc[:, 2 * e_loc :], summed[:d_loc]], axis=1).T
    conv_sum = summed[d_loc:].reshape(-1, e_loc)[:n_conv]
    n_row = taps + 1
    conv_sum = (conv_sum[:n_row] + conv_sum[n_row : 2 * n_row]) + conv_sum[2 * n_row :]
    tap_grads = conv_sum[:taps]
    bias_grads = conv_sum[taps]
    return (output, grad_tokens, grad_in_weight, grad_out_weight, tap_grads, bias_grads)


def solution(mesh):
    n_core = 2
    devices = mesh.devices.reshape(mesh.devices.shape[0] // n_core, n_core, mesh.devices.shape[1])
    split_mesh = jax.sharding.Mesh(devices, ("chip", "core", "seq"))
    return jax.shard_map(
        on_device,
        mesh=split_mesh,
        in_specs=(
            P("seq", DP),
            P(None, "seq", DP),
            P(None, DP),
            P(DP),
            P(DP, "seq"),
            P("seq", DP),
        ),
        out_specs=(
            P("seq", DP),
            P("seq", DP),
            P(None, "seq", DP),
            P(DP, "seq"),
            P(None, DP),
            P(DP),
        ),
        check_vma=False,
    )
```

```python
import jax
import jax.numpy as jnp
from jax import lax
from jax.sharding import PartitionSpec as P


DP = ("chip", "core")


def from_behind(block, axis, distance):
    devices = range(lax.axis_size(axis))
    route = [(i - distance, i) for i in devices if i - distance in devices]
    return lax.ppermute(block, axis, route)


def silu_parts(value):
    sig = jax.nn.sigmoid(value)
    return (value * sig, sig * (1.0 + value * (1.0 - sig)))


def gather_over(block, axis, n, dim):
    rep = jnp.broadcast_to(block[None], (n,) + block.shape)
    return lax.all_to_all(rep, axis, 0, dim + 1, tiled=True)[0]


def split_exact(value):
    hi = value.astype(jnp.bfloat16)
    rest = value - hi.astype(jnp.float32)
    mid = rest.astype(jnp.bfloat16)
    lo = (rest - mid.astype(jnp.float32)).astype(jnp.bfloat16)
    return jnp.concatenate([hi, mid, lo], axis=0)


def reduce_over_dp(part, n_chip, n_core):
    split = part.astype(jnp.bfloat16)
    split = split.reshape((n_chip, n_core, part.shape[0] // (n_chip * n_core)) + part.shape[1:])
    split = lax.all_to_all(split, "core", 1, 1, tiled=True).astype(jnp.float32).sum(axis=1)
    split = split.astype(jnp.bfloat16)
    return lax.all_to_all(split, "chip", 0, 0, tiled=True).astype(jnp.float32).sum(axis=0)


def on_device(tokens, in_weight, conv_weight, conv_bias, out_weight, grad_out):
    n_seq = lax.axis_size("seq")
    n_chip = lax.axis_size("chip")
    n_core = lax.axis_size("core")
    n_dp = n_chip * n_core
    w_local = jnp.concatenate([in_weight, out_weight.T[None]], axis=0)
    w_full = lax.all_gather(w_local, "seq", axis=1, tiled=True)
    in_full = w_full[:2]
    out_full_t = w_full[2]
    acts = gather_over(jnp.stack([tokens, grad_out], axis=1), "chip", n_chip, 2)
    acts = gather_over(acts.reshape(acts.shape[:2] + (n_chip, 1, -1)), "core", n_core, 3)
    acts = acts.reshape(acts.shape[:2] + (-1,))
    whole = acts[:, 0]
    upstream = acts[:, 1]
    tok_rows = whole.shape[0]
    taps = conv_weight.shape[0]
    mixed = jnp.einsum("td,pde->tpe", whole, in_full, preferred_element_type=jnp.float32).astype(
        jnp.bfloat16
    )
    inner = mixed[:, 0, :]
    gate_in = mixed[:, 1, :]
    rim = from_behind(inner[tok_rows - (taps - 1) :], "seq", 1)
    padded = jnp.concatenate([rim, inner], axis=0)
    conv = jnp.broadcast_to(conv_bias.astype(jnp.float32)[None, :], inner.shape)
    for lag in range(taps):
        conv = conv + conv_weight[lag].astype(jnp.float32)[None, :] * padded[
            lag : lag + tok_rows
        ].astype(jnp.float32)
    act, act_slope = silu_parts(conv)
    gate, gate_slope = silu_parts(gate_in.astype(jnp.float32))
    hidden = (act * gate).astype(jnp.bfloat16)
    out_part = jnp.einsum("te,de->dt", hidden, out_full_t, preferred_element_type=jnp.float32)
    back = jnp.einsum("td,de->te", upstream, out_full_t, preferred_element_type=jnp.float32)
    grad_conv = (back * gate * act_slope).astype(jnp.bfloat16)
    grad_gate = (back * act * gate_slope).astype(jnp.bfloat16)
    ahead_rim = from_behind(grad_conv[: taps - 1], "seq", -1)
    ahead = jnp.concatenate([grad_conv, ahead_rim], axis=0)
    grad_inner = jnp.zeros(inner.shape, jnp.float32)
    for lag in range(taps):
        shift_start = taps - 1 - lag
        grad_inner = grad_inner + conv_weight[lag].astype(jnp.float32)[None, :] * ahead[
            shift_start : shift_start + tok_rows
        ].astype(jnp.float32)
    grad_inner = grad_inner.astype(jnp.bfloat16)
    conv_float = grad_conv.astype(jnp.float32)
    tap_rows = []
    for lag in range(taps):
        tap_rows.append(
            jnp.sum(conv_float * padded[lag : lag + tok_rows].astype(jnp.float32), axis=0)
        )
    conv_grads = jnp.concatenate([jnp.stack(tap_rows, axis=0), jnp.sum(conv_float, axis=0)[None]], axis=0)
    branch_grads = jnp.stack([grad_inner, grad_gate], axis=1)
    tok_part = jnp.einsum("tpe,pde->dt", branch_grads, in_full, preferred_element_type=jnp.float32)
    reduced = reduce_over_dp(jnp.stack([out_part, tok_part], axis=1), n_chip, n_core)
    output = reduced[:, 0].T.astype(jnp.bfloat16)
    grad_tokens = reduced[:, 1].T.astype(jnp.bfloat16)
    term_in = jnp.einsum("td,tpe->dpe", whole, branch_grads, preferred_element_type=jnp.float32)
    term_out_t = jnp.einsum("td,te->de", upstream, hidden, preferred_element_type=jnp.float32)
    d_full, e_loc = term_out_t.shape
    d_loc = d_full // n_seq
    half = e_loc // 2
    on_sc = jnp.concatenate(
        [term_in.reshape(d_full, 2 * e_loc), term_out_t[:, :half]], axis=1
    ).astype(jnp.bfloat16)
    on_sc = lax.psum_scatter(on_sc, "seq", scatter_dimension=0, tiled=True).astype(jnp.float32)
    grad_in_weight = on_sc[:, : 2 * e_loc].reshape(d_loc, 2, e_loc).transpose(1, 0, 2)
    sent = term_out_t[:, half:].astype(jnp.bfloat16).reshape(n_seq, d_loc, e_loc - half)
    conv_parts = split_exact(conv_grads)
    n_conv = conv_parts.shape[0]
    pad_rows = (-n_conv) % 8
    conv_parts = jnp.concatenate([conv_parts, jnp.zeros((pad_rows, e_loc), jnp.bfloat16)], axis=0)
    conv_parts = conv_parts.reshape(-1, e_loc - half)
    conv_parts = jnp.broadcast_to(conv_parts[None], (n_seq,) + conv_parts.shape)
    sent = jnp.concatenate([sent, conv_parts], axis=1)
    summed = lax.all_to_all(sent, "seq", 0, 0, tiled=True).astype(jnp.float32).sum(axis=0)
    grad_out_weight = jnp.concatenate([on_sc[:, 2 * e_loc :], summed[:d_loc]], axis=1).T
    conv_sum = summed[d_loc:].reshape(-1, e_loc)[:n_conv]
    n_row = taps + 1
    conv_sum = (conv_sum[:n_row] + conv_sum[n_row : 2 * n_row]) + conv_sum[2 * n_row :]
    tap_grads = conv_sum[:taps]
    bias_grads = conv_sum[taps]
    return (output, grad_tokens, grad_in_weight, grad_out_weight, tap_grads, bias_grads)


def solution(mesh):
    n_core = 2
    devices = mesh.devices.reshape(mesh.devices.shape[0] // n_core, n_core, mesh.devices.shape[1])
    split_mesh = jax.sharding.Mesh(devices, ("chip", "core", "seq"))
    return jax.shard_map(
        on_device,
        mesh=split_mesh,
        in_specs=(
            P("seq", DP),
            P(None, "seq", DP),
            P(None, DP),
            P(DP),
            P(DP, "seq"),
            P("seq", DP),
        ),
        out_specs=(
            P("seq", DP),
            P("seq", DP),
            P(None, "seq", DP),
            P(DP, "seq"),
            P(None, DP),
            P(DP),
        ),
        check_vma=False,
    )
```

```python
import jax
import jax.numpy as jnp
from jax import lax
from jax.sharding import PartitionSpec as P


DP = ("chip", "core")


def from_behind(block, axis, distance):
    devices = range(lax.axis_size(axis))
    route = [(i - distance, i) for i in devices if i - distance in devices]
    return lax.ppermute(block, axis, route)


def silu_parts(value):
    sig = jax.nn.sigmoid(value)
    return (value * sig, sig * (1.0 + value * (1.0 - sig)))


def gather_over(block, axis, n, dim):
    rep = jnp.broadcast_to(block[None], (n,) + block.shape)
    return lax.all_to_all(rep, axis, 0, dim + 1, tiled=True)[0]


def split_exact(value):
    hi = value.astype(jnp.bfloat16)
    rest = value - hi.astype(jnp.float32)
    mid = rest.astype(jnp.bfloat16)
    lo = (rest - mid.astype(jnp.float32)).astype(jnp.bfloat16)
    return jnp.concatenate([hi, mid, lo], axis=0)


def reduce_over_dp(part, n_chip, n_core):
    split = part.reshape((n_chip, n_core, part.shape[0] // (n_chip * n_core)) + part.shape[1:])
    split = lax.all_to_all(split, "core", 1, 1, tiled=True).sum(axis=1)
    split = split.astype(jnp.bfloat16)
    return lax.all_to_all(split, "chip", 0, 0, tiled=True).astype(jnp.float32).sum(axis=0)


def on_device(tokens, in_weight, conv_weight, conv_bias, out_weight, grad_out):
    n_seq = lax.axis_size("seq")
    n_chip = lax.axis_size("chip")
    n_core = lax.axis_size("core")
    n_dp = n_chip * n_core
    w_local = jnp.concatenate([in_weight, out_weight.T[None]], axis=0)
    w_full = lax.all_gather(w_local, "seq", axis=1, tiled=True)
    in_full = w_full[:2]
    out_full_t = w_full[2]
    acts = gather_over(jnp.stack([tokens, grad_out], axis=1), "chip", n_chip, 2)
    acts = gather_over(acts.reshape(acts.shape[:2] + (n_chip, 1, -1)), "core", n_core, 3)
    acts = acts.reshape(acts.shape[:2] + (-1,))
    whole = acts[:, 0]
    upstream = acts[:, 1]
    tok_rows = whole.shape[0]
    taps = conv_weight.shape[0]
    mixed = jnp.einsum("td,pde->tpe", whole, in_full, preferred_element_type=jnp.float32).astype(
        jnp.bfloat16
    )
    inner = mixed[:, 0, :]
    gate_in = mixed[:, 1, :]
    rim = from_behind(inner[tok_rows - (taps - 1) :], "seq", 1)
    padded = jnp.concatenate([rim, inner], axis=0)
    conv = jnp.broadcast_to(conv_bias.astype(jnp.float32)[None, :], inner.shape)
    for lag in range(taps):
        conv = conv + conv_weight[lag].astype(jnp.float32)[None, :] * padded[
            lag : lag + tok_rows
        ].astype(jnp.float32)
    act, act_slope = silu_parts(conv)
    gate, gate_slope = silu_parts(gate_in.astype(jnp.float32))
    hidden = (act * gate).astype(jnp.bfloat16)
    out_part = jnp.einsum("te,de->dt", hidden, out_full_t, preferred_element_type=jnp.float32)
    back = jnp.einsum("td,de->te", upstream, out_full_t, preferred_element_type=jnp.float32)
    grad_conv = (back * gate * act_slope).astype(jnp.bfloat16)
    grad_gate = (back * act * gate_slope).astype(jnp.bfloat16)
    ahead_rim = from_behind(grad_conv[: taps - 1], "seq", -1)
    ahead = jnp.concatenate([grad_conv, ahead_rim], axis=0)
    grad_inner = jnp.zeros(inner.shape, jnp.float32)
    for lag in range(taps):
        shift_start = taps - 1 - lag
        grad_inner = grad_inner + conv_weight[lag].astype(jnp.float32)[None, :] * ahead[
            shift_start : shift_start + tok_rows
        ].astype(jnp.float32)
    grad_inner = grad_inner.astype(jnp.bfloat16)
    conv_float = grad_conv.astype(jnp.float32)
    tap_rows = []
    for lag in range(taps):
        tap_rows.append(
            jnp.sum(conv_float * padded[lag : lag + tok_rows].astype(jnp.float32), axis=0)
        )
    conv_grads = jnp.concatenate([jnp.stack(tap_rows, axis=0), jnp.sum(conv_float, axis=0)[None]], axis=0)
    branch_grads = jnp.stack([grad_inner, grad_gate], axis=1)
    tok_part = jnp.einsum("tpe,pde->dt", branch_grads, in_full, preferred_element_type=jnp.float32)
    reduced = reduce_over_dp(jnp.stack([out_part, tok_part], axis=1), n_chip, n_core)
    output = reduced[:, 0].T.astype(jnp.bfloat16)
    grad_tokens = reduced[:, 1].T.astype(jnp.bfloat16)
    term_in = jnp.einsum("td,tpe->pde", whole, branch_grads, preferred_element_type=jnp.float32)
    term_out_t = jnp.einsum("td,te->de", upstream, hidden, preferred_element_type=jnp.float32)
    terms = jnp.concatenate([term_in, term_out_t[None]], axis=0).astype(jnp.bfloat16)
    terms = lax.psum_scatter(terms, "seq", scatter_dimension=1, tiled=True).astype(jnp.float32)
    grad_in_weight = terms[:2]
    grad_out_weight = terms[2].T
    conv_parts = split_exact(conv_grads)
    conv_parts = jnp.broadcast_to(conv_parts[None], (n_seq,) + conv_parts.shape)
    parts = lax.all_to_all(conv_parts, "seq", 0, 0, tiled=True).astype(jnp.float32).sum(axis=0)
    n_row = taps + 1
    conv_grads = (parts[:n_row] + parts[n_row : 2 * n_row]) + parts[2 * n_row :]
    tap_grads = conv_grads[:taps]
    bias_grads = conv_grads[taps]
    return (output, grad_tokens, grad_in_weight, grad_out_weight, tap_grads, bias_grads)


def solution(mesh):
    n_core = 2
    devices = mesh.devices.reshape(mesh.devices.shape[0] // n_core, n_core, mesh.devices.shape[1])
    split_mesh = jax.sharding.Mesh(devices, ("chip", "core", "seq"))
    return jax.shard_map(
        on_device,
        mesh=split_mesh,
        in_specs=(
            P("seq", DP),
            P(None, "seq", DP),
            P(None, DP),
            P(DP),
            P(DP, "seq"),
            P("seq", DP),
        ),
        out_specs=(
            P("seq", DP),
            P("seq", DP),
            P(None, "seq", DP),
            P(DP, "seq"),
            P(None, DP),
            P(DP),
        ),
        check_vma=False,
    )
```

```python
import jax
import jax.numpy as jnp
from jax import lax
from jax.sharding import PartitionSpec as P


DP = ("chip", "core")


def from_behind(block, axis, distance):
    devices = range(lax.axis_size(axis))
    route = [(i - distance, i) for i in devices if i - distance in devices]
    return lax.ppermute(block, axis, route)


def silu_parts(value):
    sig = jax.nn.sigmoid(value)
    return (value * sig, sig * (1.0 + value * (1.0 - sig)))


def gather_over(block, axis, n, dim):
    rep = jnp.broadcast_to(block[None], (n,) + block.shape)
    return lax.all_to_all(rep, axis, 0, dim + 1, tiled=True)[0]


def split_exact(value):
    hi = value.astype(jnp.bfloat16)
    rest = value - hi.astype(jnp.float32)
    mid = rest.astype(jnp.bfloat16)
    lo = (rest - mid.astype(jnp.float32)).astype(jnp.bfloat16)
    return jnp.concatenate([hi, mid, lo], axis=0)


def reduce_over_dp(part, n_chip, n_core):
    split = part.astype(jnp.bfloat16)
    split = split.reshape((n_chip, n_core, part.shape[0] // (n_chip * n_core)) + part.shape[1:])
    split = lax.all_to_all(split, "core", 1, 1, tiled=True).astype(jnp.float32).sum(axis=1)
    split = split.astype(jnp.bfloat16)
    return lax.all_to_all(split, "chip", 0, 0, tiled=True).astype(jnp.float32).sum(axis=0)


def on_device(tokens, in_weight, conv_weight, conv_bias, out_weight, grad_out):
    n_seq = lax.axis_size("seq")
    n_chip = lax.axis_size("chip")
    n_core = lax.axis_size("core")
    n_dp = n_chip * n_core
    w_local = jnp.concatenate([in_weight, out_weight.T[None]], axis=0)
    w_full = lax.all_gather(w_local, "seq", axis=1, tiled=True)
    in_full = w_full[:2]
    out_full_t = w_full[2]
    acts = gather_over(jnp.stack([tokens, grad_out], axis=1), "chip", n_chip, 2)
    acts = gather_over(acts.reshape(acts.shape[:2] + (n_chip, 1, -1)), "core", n_core, 3)
    acts = acts.reshape(acts.shape[:2] + (-1,))
    whole = acts[:, 0]
    upstream = acts[:, 1]
    tok_rows = whole.shape[0]
    taps = conv_weight.shape[0]
    mixed = jnp.einsum("td,pde->tpe", whole, in_full, preferred_element_type=jnp.float32).astype(
        jnp.bfloat16
    )
    inner = mixed[:, 0, :]
    gate_in = mixed[:, 1, :]
    rim = from_behind(inner[tok_rows - (taps - 1) :], "seq", 1)
    padded = jnp.concatenate([rim, inner], axis=0)
    conv = jnp.broadcast_to(conv_bias.astype(jnp.float32)[None, :], inner.shape)
    for lag in range(taps):
        conv = conv + conv_weight[lag].astype(jnp.float32)[None, :] * padded[
            lag : lag + tok_rows
        ].astype(jnp.float32)
    act, act_slope = silu_parts(conv)
    gate, gate_slope = silu_parts(gate_in.astype(jnp.float32))
    hidden = (act * gate).astype(jnp.bfloat16)
    out_part = jnp.einsum("te,de->dt", hidden, out_full_t, preferred_element_type=jnp.float32)
    back = jnp.einsum("td,de->te", upstream, out_full_t, preferred_element_type=jnp.float32)
    grad_conv = (back * gate * act_slope).astype(jnp.bfloat16)
    grad_gate = (back * act * gate_slope).astype(jnp.bfloat16)
    ahead_rim = from_behind(grad_conv[: taps - 1], "seq", -1)
    ahead = jnp.concatenate([grad_conv, ahead_rim], axis=0)
    grad_inner = jnp.zeros(inner.shape, jnp.float32)
    for lag in range(taps):
        shift_start = taps - 1 - lag
        grad_inner = grad_inner + conv_weight[lag].astype(jnp.float32)[None, :] * ahead[
            shift_start : shift_start + tok_rows
        ].astype(jnp.float32)
    grad_inner = grad_inner.astype(jnp.bfloat16)
    conv_float = grad_conv.astype(jnp.float32)
    tap_rows = []
    for lag in range(taps):
        tap_rows.append(
            jnp.sum(conv_float * padded[lag : lag + tok_rows].astype(jnp.float32), axis=0)
        )
    conv_grads = jnp.concatenate([jnp.stack(tap_rows, axis=0), jnp.sum(conv_float, axis=0)[None]], axis=0)
    branch_grads = jnp.stack([grad_inner, grad_gate], axis=1)
    tok_part = jnp.einsum("tpe,pde->dt", branch_grads, in_full, preferred_element_type=jnp.float32)
    reduced = reduce_over_dp(jnp.stack([out_part, tok_part], axis=1), n_chip, n_core)
    output = reduced[:, 0].T.astype(jnp.bfloat16)
    grad_tokens = reduced[:, 1].T.astype(jnp.bfloat16)
    term_in = jnp.einsum("td,tpe->pde", whole, branch_grads, preferred_element_type=jnp.float32)
    term_out_t = jnp.einsum("td,te->de", upstream, hidden, preferred_element_type=jnp.float32)
    terms = jnp.concatenate([term_in, term_out_t[None]], axis=0).astype(jnp.bfloat16)
    terms = lax.psum_scatter(terms, "seq", scatter_dimension=1, tiled=True).astype(jnp.float32)
    grad_in_weight = terms[:2]
    grad_out_weight = terms[2].T
    conv_parts = split_exact(conv_grads)
    conv_parts = jnp.broadcast_to(conv_parts[None], (n_seq,) + conv_parts.shape)
    parts = lax.all_to_all(conv_parts, "seq", 0, 0, tiled=True).astype(jnp.float32).sum(axis=0)
    n_row = taps + 1
    conv_grads = (parts[:n_row] + parts[n_row : 2 * n_row]) + parts[2 * n_row :]
    tap_grads = conv_grads[:taps]
    bias_grads = conv_grads[taps]
    return (output, grad_tokens, grad_in_weight, grad_out_weight, tap_grads, bias_grads)


def solution(mesh):
    n_core = 2
    devices = mesh.devices.reshape(mesh.devices.shape[0] // n_core, n_core, mesh.devices.shape[1])
    split_mesh = jax.sharding.Mesh(devices, ("chip", "core", "seq"))
    return jax.shard_map(
        on_device,
        mesh=split_mesh,
        in_specs=(
            P("seq", DP),
            P(None, "seq", DP),
            P(None, DP),
            P(DP),
            P(DP, "seq"),
            P("seq", DP),
        ),
        out_specs=(
            P("seq", DP),
            P("seq", DP),
            P(None, "seq", DP),
            P(DP, "seq"),
            P(None, DP),
            P(DP),
        ),
        check_vma=False,
    )
```

```python
import jax
import jax.numpy as jnp
from jax import lax
from jax.sharding import PartitionSpec as P


DP = ("chip", "core")


def from_behind(block, axis, distance):
    devices = range(lax.axis_size(axis))
    route = [(i - distance, i) for i in devices if i - distance in devices]
    return lax.ppermute(block, axis, route)


def silu_parts(value):
    sig = jax.nn.sigmoid(value)
    return (value * sig, sig * (1.0 + value * (1.0 - sig)))


def gather_over(block, axis, n, dim):
    rep = jnp.broadcast_to(block[None], (n,) + block.shape)
    return lax.all_to_all(rep, axis, 0, dim + 1, tiled=True)[0]


def split_exact(value):
    hi = value.astype(jnp.bfloat16)
    rest = value - hi.astype(jnp.float32)
    mid = rest.astype(jnp.bfloat16)
    lo = (rest - mid.astype(jnp.float32)).astype(jnp.bfloat16)
    return jnp.concatenate([hi, mid, lo], axis=0)


def reduce_over_dp(part, n_chip, n_core):
    split = part.astype(jnp.bfloat16)
    split = split.reshape((n_chip, n_core, part.shape[0] // (n_chip * n_core)) + part.shape[1:])
    split = lax.all_to_all(split, "core", 1, 1, tiled=True).astype(jnp.float32).sum(axis=1)
    split = split.astype(jnp.bfloat16)
    return lax.all_to_all(split, "chip", 0, 0, tiled=True).astype(jnp.float32).sum(axis=0)


def on_device(tokens, in_weight, conv_weight, conv_bias, out_weight, grad_out):
    n_seq = lax.axis_size("seq")
    n_chip = lax.axis_size("chip")
    n_core = lax.axis_size("core")
    n_dp = n_chip * n_core
    w_local = jnp.concatenate([in_weight, out_weight.T[None]], axis=0)
    w_full = lax.all_gather(w_local, "seq", axis=1, tiled=True)
    in_full = w_full[:2]
    out_full_t = w_full[2]
    taps = conv_weight.shape[0]
    rim_rows = taps - 1
    tok_rows = tokens.shape[0]
    ext_tok = jnp.concatenate(
        [
            from_behind(tokens[tok_rows - rim_rows :], "seq", 1),
            tokens,
            from_behind(tokens[:rim_rows], "seq", -1),
        ],
        axis=0,
    )
    ext_go = jnp.concatenate(
        [jnp.zeros_like(grad_out[:rim_rows]), grad_out, from_behind(grad_out[:rim_rows], "seq", -1)],
        axis=0,
    )
    acts = gather_over(jnp.stack([ext_tok, ext_go], axis=1), "chip", n_chip, 2)
    acts = gather_over(acts.reshape(acts.shape[:2] + (n_chip, 1, -1)), "core", n_core, 3)
    acts = acts.reshape(acts.shape[:2] + (-1,))
    whole = acts[rim_rows : rim_rows + tok_rows, 0]
    upstream_ext = acts[rim_rows:, 1]
    upstream = upstream_ext[:tok_rows]
    mixed = jnp.einsum("td,pde->tpe", acts[:, 0], in_full, preferred_element_type=jnp.float32).astype(
        jnp.bfloat16
    )
    inner_ext = mixed[:, 0, :]
    gate_in = mixed[rim_rows:, 1, :]
    n_out = tok_rows + rim_rows
    conv = jnp.broadcast_to(conv_bias.astype(jnp.float32)[None, :], (n_out, inner_ext.shape[1]))
    for lag in range(taps):
        conv = conv + conv_weight[lag].astype(jnp.float32)[None, :] * inner_ext[
            lag : lag + n_out
        ].astype(jnp.float32)
    act, act_slope = silu_parts(conv)
    gate, gate_slope = silu_parts(gate_in.astype(jnp.float32))
    hidden = (act[:tok_rows] * gate[:tok_rows]).astype(jnp.bfloat16)
    out_part = jnp.einsum("te,de->dt", hidden, out_full_t, preferred_element_type=jnp.float32)
    back = jnp.einsum("td,de->te", upstream_ext, out_full_t, preferred_element_type=jnp.float32)
    ahead = (back * gate * act_slope).astype(jnp.bfloat16)
    grad_conv = ahead[:tok_rows]
    grad_gate = (back[:tok_rows] * act[:tok_rows] * gate_slope[:tok_rows]).astype(jnp.bfloat16)
    padded = inner_ext[:n_out]
    inner = inner_ext[rim_rows : rim_rows + tok_rows]
    grad_inner = jnp.zeros(inner.shape, jnp.float32)
    for lag in range(taps):
        shift_start = taps - 1 - lag
        grad_inner = grad_inner + conv_weight[lag].astype(jnp.float32)[None, :] * ahead[
            shift_start : shift_start + tok_rows
        ].astype(jnp.float32)
    grad_inner = grad_inner.astype(jnp.bfloat16)
    conv_float = grad_conv.astype(jnp.float32)
    tap_rows = []
    for lag in range(taps):
        tap_rows.append(
            jnp.sum(conv_float * padded[lag : lag + tok_rows].astype(jnp.float32), axis=0)
        )
    conv_grads = jnp.concatenate([jnp.stack(tap_rows, axis=0), jnp.sum(conv_float, axis=0)[None]], axis=0)
    branch_grads = jnp.stack([grad_inner, grad_gate], axis=1)
    tok_part = jnp.einsum("tpe,pde->dt", branch_grads, in_full, preferred_element_type=jnp.float32)
    reduced = reduce_over_dp(jnp.stack([out_part, tok_part], axis=1), n_chip, n_core)
    output = reduced[:, 0].T.astype(jnp.bfloat16)
    grad_tokens = reduced[:, 1].T.astype(jnp.bfloat16)
    term_in = jnp.einsum("td,tpe->pde", whole, branch_grads, preferred_element_type=jnp.float32)
    term_out_t = jnp.einsum("td,te->de", upstream, hidden, preferred_element_type=jnp.float32)
    terms = jnp.concatenate([term_in, term_out_t[None]], axis=0).astype(jnp.bfloat16)
    terms = lax.psum_scatter(terms, "seq", scatter_dimension=1, tiled=True).astype(jnp.float32)
    grad_in_weight = terms[:2]
    grad_out_weight = terms[2].T
    conv_parts = split_exact(conv_grads)
    conv_parts = jnp.broadcast_to(conv_parts[None], (n_seq,) + conv_parts.shape)
    parts = lax.all_to_all(conv_parts, "seq", 0, 0, tiled=True).astype(jnp.float32).sum(axis=0)
    n_row = taps + 1
    conv_grads = (parts[:n_row] + parts[n_row : 2 * n_row]) + parts[2 * n_row :]
    tap_grads = conv_grads[:taps]
    bias_grads = conv_grads[taps]
    return (output, grad_tokens, grad_in_weight, grad_out_weight, tap_grads, bias_grads)


def solution(mesh):
    n_core = 2
    devices = mesh.devices.reshape(mesh.devices.shape[0] // n_core, n_core, mesh.devices.shape[1])
    split_mesh = jax.sharding.Mesh(devices, ("chip", "core", "seq"))
    return jax.shard_map(
        on_device,
        mesh=split_mesh,
        in_specs=(
            P("seq", DP),
            P(None, "seq", DP),
            P(None, DP),
            P(DP),
            P(DP, "seq"),
            P("seq", DP),
        ),
        out_specs=(
            P("seq", DP),
            P("seq", DP),
            P(None, "seq", DP),
            P(DP, "seq"),
            P(None, DP),
            P(DP),
        ),
        check_vma=False,
    )
```

```python
import jax
import jax.numpy as jnp
from jax import lax
from jax.sharding import PartitionSpec as P


DP = ("chip", "core")


def from_behind(block, axis, distance):
    devices = range(lax.axis_size(axis))
    route = [(i - distance, i) for i in devices if i - distance in devices]
    return lax.ppermute(block, axis, route)


def silu_parts(value):
    sig = jax.nn.sigmoid(value)
    return (value * sig, sig * (1.0 + value * (1.0 - sig)))


def gather_over(block, axis, n, dim):
    rep = jnp.broadcast_to(block[None], (n,) + block.shape)
    return lax.all_to_all(rep, axis, 0, dim + 1, tiled=True)[0]


def split_exact(value):
    hi = value.astype(jnp.bfloat16)
    rest = value - hi.astype(jnp.float32)
    mid = rest.astype(jnp.bfloat16)
    lo = (rest - mid.astype(jnp.float32)).astype(jnp.bfloat16)
    return jnp.concatenate([hi, mid, lo], axis=0)


def reduce_over_dp(part, n_chip, n_core):
    split = part.astype(jnp.bfloat16)
    split = split.reshape((n_chip, n_core, part.shape[0] // (n_chip * n_core)) + part.shape[1:])
    split = lax.all_to_all(split, "core", 1, 1, tiled=True).astype(jnp.float32).sum(axis=1)
    split = split.astype(jnp.bfloat16)
    return lax.all_to_all(split, "chip", 0, 0, tiled=True).astype(jnp.float32).sum(axis=0)


def on_device(tokens, in_weight, conv_weight, conv_bias, out_weight, grad_out):
    n_seq = lax.axis_size("seq")
    n_chip = lax.axis_size("chip")
    n_core = lax.axis_size("core")
    n_dp = n_chip * n_core
    w_local = jnp.concatenate([in_weight, out_weight.T[None]], axis=0)
    w_full = lax.all_gather(w_local, "seq", axis=1, tiled=True)
    in_full = w_full[:2]
    out_full_t = w_full[2]
    taps = conv_weight.shape[0]
    rim_rows = taps - 1
    halo = 8
    base = halo - rim_rows
    tok_rows = tokens.shape[0]
    ext_tok = jnp.concatenate(
        [
            from_behind(tokens[tok_rows - halo :], "seq", 1),
            tokens,
            from_behind(tokens[:halo], "seq", -1),
        ],
        axis=0,
    )
    ext_go = jnp.concatenate(
        [jnp.zeros_like(grad_out[:halo]), grad_out, from_behind(grad_out[:halo], "seq", -1)],
        axis=0,
    )
    acts = gather_over(jnp.stack([ext_tok, ext_go], axis=1), "chip", n_chip, 2)
    acts = gather_over(acts.reshape(acts.shape[:2] + (n_chip, 1, -1)), "core", n_core, 3)
    acts = acts.reshape(acts.shape[:2] + (-1,))
    n_out = tok_rows + rim_rows
    whole = acts[halo : halo + tok_rows, 0]
    upstream_ext = acts[halo : halo + n_out, 1]
    upstream = upstream_ext[:tok_rows]
    mixed = jnp.einsum("td,pde->tpe", acts[:, 0], in_full, preferred_element_type=jnp.float32).astype(
        jnp.bfloat16
    )
    inner_ext = mixed[base:, 0, :]
    gate_in = mixed[halo : halo + n_out, 1, :]
    conv = jnp.broadcast_to(conv_bias.astype(jnp.float32)[None, :], (n_out, inner_ext.shape[1]))
    for lag in range(taps):
        conv = conv + conv_weight[lag].astype(jnp.float32)[None, :] * inner_ext[
            lag : lag + n_out
        ].astype(jnp.float32)
    act, act_slope = silu_parts(conv)
    gate, gate_slope = silu_parts(gate_in.astype(jnp.float32))
    hidden = (act[:tok_rows] * gate[:tok_rows]).astype(jnp.bfloat16)
    out_part = jnp.einsum("te,de->dt", hidden, out_full_t, preferred_element_type=jnp.float32)
    back = jnp.einsum("td,de->te", upstream_ext, out_full_t, preferred_element_type=jnp.float32)
    ahead = (back * gate * act_slope).astype(jnp.bfloat16)
    grad_conv = ahead[:tok_rows]
    grad_gate = (back[:tok_rows] * act[:tok_rows] * gate_slope[:tok_rows]).astype(jnp.bfloat16)
    padded = inner_ext[:n_out]
    inner = inner_ext[rim_rows : rim_rows + tok_rows]
    grad_inner = jnp.zeros(inner.shape, jnp.float32)
    for lag in range(taps):
        shift_start = taps - 1 - lag
        grad_inner = grad_inner + conv_weight[lag].astype(jnp.float32)[None, :] * ahead[
            shift_start : shift_start + tok_rows
        ].astype(jnp.float32)
    grad_inner = grad_inner.astype(jnp.bfloat16)
    conv_float = grad_conv.astype(jnp.float32)
    tap_rows = []
    for lag in range(taps):
        tap_rows.append(
            jnp.sum(conv_float * padded[lag : lag + tok_rows].astype(jnp.float32), axis=0)
        )
    conv_grads = jnp.concatenate([jnp.stack(tap_rows, axis=0), jnp.sum(conv_float, axis=0)[None]], axis=0)
    branch_grads = jnp.stack([grad_inner, grad_gate], axis=1)
    tok_part = jnp.einsum("tpe,pde->dt", branch_grads, in_full, preferred_element_type=jnp.float32)
    reduced = reduce_over_dp(jnp.stack([out_part, tok_part], axis=1), n_chip, n_core)
    output = reduced[:, 0].T.astype(jnp.bfloat16)
    grad_tokens = reduced[:, 1].T.astype(jnp.bfloat16)
    term_in = jnp.einsum("td,tpe->pde", whole, branch_grads, preferred_element_type=jnp.float32)
    term_out_t = jnp.einsum("td,te->de", upstream, hidden, preferred_element_type=jnp.float32)
    terms = jnp.concatenate([term_in, term_out_t[None]], axis=0).astype(jnp.bfloat16)
    terms = lax.psum_scatter(terms, "seq", scatter_dimension=1, tiled=True).astype(jnp.float32)
    grad_in_weight = terms[:2]
    grad_out_weight = terms[2].T
    conv_parts = split_exact(conv_grads)
    conv_parts = jnp.broadcast_to(conv_parts[None], (n_seq,) + conv_parts.shape)
    parts = lax.all_to_all(conv_parts, "seq", 0, 0, tiled=True).astype(jnp.float32).sum(axis=0)
    n_row = taps + 1
    conv_grads = (parts[:n_row] + parts[n_row : 2 * n_row]) + parts[2 * n_row :]
    tap_grads = conv_grads[:taps]
    bias_grads = conv_grads[taps]
    return (output, grad_tokens, grad_in_weight, grad_out_weight, tap_grads, bias_grads)


def solution(mesh):
    n_core = 2
    devices = mesh.devices.reshape(mesh.devices.shape[0] // n_core, n_core, mesh.devices.shape[1])
    split_mesh = jax.sharding.Mesh(devices, ("chip", "core", "seq"))
    return jax.shard_map(
        on_device,
        mesh=split_mesh,
        in_specs=(
            P("seq", DP),
            P(None, "seq", DP),
            P(None, DP),
            P(DP),
            P(DP, "seq"),
            P("seq", DP),
        ),
        out_specs=(
            P("seq", DP),
            P("seq", DP),
            P(None, "seq", DP),
            P(DP, "seq"),
            P(None, DP),
            P(DP),
        ),
        check_vma=False,
    )
```

```python
import jax
import jax.numpy as jnp
from jax import lax
from jax.sharding import PartitionSpec as P


DP = ("chip", "core")


def from_behind(block, axis, distance):
    devices = range(lax.axis_size(axis))
    route = [(i - distance, i) for i in devices if i - distance in devices]
    return lax.ppermute(block, axis, route)


def silu_parts(value):
    sig = jax.nn.sigmoid(value)
    return (value * sig, sig * (1.0 + value * (1.0 - sig)))


def gather_over(block, axis, n, dim):
    rep = jnp.broadcast_to(block[None], (n,) + block.shape)
    return lax.all_to_all(rep, axis, 0, dim + 1, tiled=True)[0]


def split_exact(value):
    hi = value.astype(jnp.bfloat16)
    rest = value - hi.astype(jnp.float32)
    mid = rest.astype(jnp.bfloat16)
    lo = (rest - mid.astype(jnp.float32)).astype(jnp.bfloat16)
    return jnp.concatenate([hi, mid, lo], axis=0)


def reduce_over_dp(part, n_chip, n_core):
    split = part.astype(jnp.bfloat16)
    split = split.reshape((n_chip, n_core, part.shape[0] // (n_chip * n_core)) + part.shape[1:])
    split = lax.all_to_all(split, "core", 1, 1, tiled=True).astype(jnp.float32).sum(axis=1)
    split = split.astype(jnp.bfloat16)
    return lax.all_to_all(split, "chip", 0, 0, tiled=True).astype(jnp.float32).sum(axis=0)


def on_device(tokens, in_weight, conv_weight, conv_bias, out_weight, grad_out):
    n_seq = lax.axis_size("seq")
    n_chip = lax.axis_size("chip")
    n_core = lax.axis_size("core")
    n_dp = n_chip * n_core
    w_local = jnp.concatenate([in_weight, out_weight.T[None]], axis=0)
    w_full = lax.all_gather(w_local, "seq", axis=1, tiled=True)
    in_full = w_full[:2]
    out_full_t = w_full[2]
    acts = gather_over(jnp.stack([tokens, grad_out], axis=1), "chip", n_chip, 2)
    acts = gather_over(acts.reshape(acts.shape[:2] + (n_chip, 1, -1)), "core", n_core, 3)
    acts = acts.reshape(acts.shape[:2] + (-1,))
    whole = acts[:, 0]
    upstream = acts[:, 1]
    tok_rows = whole.shape[0]
    taps = conv_weight.shape[0]
    mixed = jnp.einsum("td,pde->tpe", whole, in_full, preferred_element_type=jnp.float32).astype(
        jnp.bfloat16
    )
    inner = mixed[:, 0, :]
    gate_in = mixed[:, 1, :]
    tail = jnp.einsum(
        "td,de->te", whole[tok_rows - (taps - 1) :], in_full[0], preferred_element_type=jnp.float32
    ).astype(jnp.bfloat16)
    rim = from_behind(tail, "seq", 1)
    padded = jnp.concatenate([rim, inner], axis=0)
    conv = jnp.broadcast_to(conv_bias.astype(jnp.float32)[None, :], inner.shape)
    for lag in range(taps):
        conv = conv + conv_weight[lag].astype(jnp.float32)[None, :] * padded[
            lag : lag + tok_rows
        ].astype(jnp.float32)
    act, act_slope = silu_parts(conv)
    gate, gate_slope = silu_parts(gate_in.astype(jnp.float32))
    hidden = (act * gate).astype(jnp.bfloat16)
    out_part = jnp.einsum("te,de->dt", hidden, out_full_t, preferred_element_type=jnp.float32)
    back = jnp.einsum("td,de->te", upstream, out_full_t, preferred_element_type=jnp.float32)
    grad_conv = (back * gate * act_slope).astype(jnp.bfloat16)
    grad_gate = (back * act * gate_slope).astype(jnp.bfloat16)
    head_back = jnp.einsum(
        "td,de->te", upstream[: taps - 1], out_full_t, preferred_element_type=jnp.float32
    )
    head = (head_back * gate[: taps - 1] * act_slope[: taps - 1]).astype(jnp.bfloat16)
    ahead_rim = from_behind(head, "seq", -1)
    ahead = jnp.concatenate([grad_conv, ahead_rim], axis=0)
    grad_inner = jnp.zeros(inner.shape, jnp.float32)
    for lag in range(taps):
        shift_start = taps - 1 - lag
        grad_inner = grad_inner + conv_weight[lag].astype(jnp.float32)[None, :] * ahead[
            shift_start : shift_start + tok_rows
        ].astype(jnp.float32)
    grad_inner = grad_inner.astype(jnp.bfloat16)
    conv_float = grad_conv.astype(jnp.float32)
    tap_rows = []
    for lag in range(taps):
        tap_rows.append(
            jnp.sum(conv_float * padded[lag : lag + tok_rows].astype(jnp.float32), axis=0)
        )
    conv_grads = jnp.concatenate([jnp.stack(tap_rows, axis=0), jnp.sum(conv_float, axis=0)[None]], axis=0)
    branch_grads = jnp.stack([grad_inner, grad_gate], axis=1)
    tok_part = jnp.einsum("tpe,pde->dt", branch_grads, in_full, preferred_element_type=jnp.float32)
    reduced = reduce_over_dp(jnp.stack([out_part, tok_part], axis=1), n_chip, n_core)
    output = reduced[:, 0].T.astype(jnp.bfloat16)
    grad_tokens = reduced[:, 1].T.astype(jnp.bfloat16)
    term_in = jnp.einsum("td,tpe->pde", whole, branch_grads, preferred_element_type=jnp.float32)
    term_out_t = jnp.einsum("td,te->de", upstream, hidden, preferred_element_type=jnp.float32)
    terms = jnp.concatenate([term_in, term_out_t[None]], axis=0).astype(jnp.bfloat16)
    terms = lax.psum_scatter(terms, "seq", scatter_dimension=1, tiled=True).astype(jnp.float32)
    grad_in_weight = terms[:2]
    grad_out_weight = terms[2].T
    conv_parts = split_exact(conv_grads)
    conv_parts = jnp.broadcast_to(conv_parts[None], (n_seq,) + conv_parts.shape)
    parts = lax.all_to_all(conv_parts, "seq", 0, 0, tiled=True).astype(jnp.float32).sum(axis=0)
    n_row = taps + 1
    conv_grads = (parts[:n_row] + parts[n_row : 2 * n_row]) + parts[2 * n_row :]
    tap_grads = conv_grads[:taps]
    bias_grads = conv_grads[taps]
    return (output, grad_tokens, grad_in_weight, grad_out_weight, tap_grads, bias_grads)


def solution(mesh):
    n_core = 2
    devices = mesh.devices.reshape(mesh.devices.shape[0] // n_core, n_core, mesh.devices.shape[1])
    split_mesh = jax.sharding.Mesh(devices, ("chip", "core", "seq"))
    return jax.shard_map(
        on_device,
        mesh=split_mesh,
        in_specs=(
            P("seq", DP),
            P(None, "seq", DP),
            P(None, DP),
            P(DP),
            P(DP, "seq"),
            P("seq", DP),
        ),
        out_specs=(
            P("seq", DP),
            P("seq", DP),
            P(None, "seq", DP),
            P(DP, "seq"),
            P(None, DP),
            P(DP),
        ),
        check_vma=False,
    )
```
